128 devices in a mesh: seq: 32 (over x, z, core), tp: 4 (over y).
Axes of the slice: x: 4, y: 4, z: 4, core: 2. Of those that a mesh axis runs over, the one named last changes fastest.
Arguments:
- hidden_in: bfloat16 [4, 64, 2048], replicated, may hold values from -8 to 8
- lengths: int32 [64], replicated, may hold values from 2 to 16384, as said below
- request_perm: int32 [64], replicated, may hold values from 0 to 63, each once
- k_cache: bfloat16 [64, 16384, 512], P(None, 'seq', 'tp'), may hold values from -2450 to 2450
- v_cache: bfloat16 [64, 16384, 512], P(None, 'seq', 'tp'), may hold values from -16 to 16
- attn_gain: bfloat16 [2048], replicated, may hold values from 0.5 to 1.5
- w_query: bfloat16 [2048, 2048], P(None, 'tp'), may hold values from -0.125 to 0.125
- w_key: bfloat16 [2048, 512], P(None, 'tp'), may hold values from -2 to 2
- w_value: bfloat16 [2048, 512], P(None, 'tp'), may hold values from -0.5 to 0.5
- w_out: bfloat16 [2048, 2048], P('tp'), may hold values from -0.125 to 0.125
- mlp_gain: bfloat16 [2048], replicated, may hold values from 0.099609375 to 1.8984375
- w_gate: bfloat16 [8192, 2048], P(('seq', 'tp')), may hold values from -0.125 to 0.125
- w_up: bfloat16 [8192, 2048], P(('seq', 'tp')), may hold values from -0.125 to 0.125
- w_down: bfloat16 [8192, 2048], P(('seq', 'tp')), may hold values from -1 to 1
Outputs:
- hidden_out: bfloat16 [4, 64, 2048], replicated
- key_new: bfloat16 [4, 64, 512], P(None, None, 'tp')
- value_new: bfloat16 [4, 64, 512], P(None, None, 'tp')
The draws below stay inside these ranges and needn't reach their ends.
Inputs may be any that keep to these rules, and one draw needn't show every extreme that they name: `lengths`: some request has exactly 16384 cached positions.
All inputs are finite; a program needn't handle non-finite values.
Results may differ from the reference program's by a relative error of at most 0.014.
The reference program's roundings to bfloat16 on the way count: a program that leaves them out, or rounds other values in their place, can miss the bound.
Values may be sent and summed in bfloat16 or wider, within the bound.
No kernel may reach another device: no remote copies, remote signals or barrier semaphores. Data moves between devices by JAX's collectives and lax.ppermute only.
A program may use at most 192 MiB of HBM per device.

```python
import math
import jax
import jax.numpy as jnp
from jax import lax

D = 2048
H = 32
KVH = 8
HD = 64
FF = 8192
R = 64
STEPS = 4
S_CAP = 16384


def draw_lengths(key, part):
    key_list = jax.random.split(key, 3)
    first_draw = jax.random.randint(key_list[0], (R,), 0, S_CAP - 1)
    second_draw = jax.random.randint(key_list[1], (R,), 0, S_CAP - 1)
    drawn_lengths = 2 + first_draw * second_draw // S_CAP
    longest = jax.random.randint(key_list[2], (), 0, R)
    return drawn_lengths.at[longest].set(S_CAP).astype(jnp.int32)


def draw_hidden_in(key, part):
    key_list = jax.random.split(key, 3)
    full_shape = (STEPS, R, D)
    row_scale = jnp.exp(jax.random.uniform(key_list[1], (STEPS, R, 1), jnp.float32, math.log(0.3), 0.0))
    column_scale = jnp.exp(jax.random.uniform(key_list[2], (1, 1, D), jnp.float32, math.log(0.5), math.log(2.0)))
    core_values = jax.random.truncated_normal(key_list[0], -4.0, 4.0, full_shape, jnp.float32)
    return (core_values * row_scale * column_scale).astype(jnp.bfloat16)


def draw_k_cache(key, part):
    key_list = jax.random.split(key, 1)
    full_shape = (R, S_CAP, KVH * HD)
    base_values = 16.0 * jax.random.truncated_normal(key_list[0], -4.0, 4.0, full_shape, jnp.float32)
    return base_values.astype(jnp.bfloat16)


def raised(entries, rng, source, target, blocks, factor):
    def block_of(position):
        return (jnp.arange(entries.shape[position]) // (entries.shape[position] // blocks)).reshape((-1,) + (1,) * (entries.ndim - 1 - position))

    one_side = jax.random.permutation(rng, blocks)[block_of(target)]
    far = (block_of(target) + blocks // 2) % blocks
    return jnp.where((block_of(source) == one_side) | (block_of(source) == far), factor * entries, entries)


def steps_of(rng, dims, cuts, smallest, high):
    loudness, own = 1.0, jax.random.fold_in(rng, 6)
    for axis_at, parts in cuts:
        steps = jnp.exp(jax.random.uniform(jax.random.fold_in(own, axis_at), (parts,), jnp.float32, smallest / len(cuts), high / len(cuts)))
        loudness = loudness * jnp.repeat(steps, dims[axis_at] // parts).reshape([-1 if axis == axis_at else 1 for axis in range(len(dims))])
    return loudness


def scatter_about(own_key, dims, spread, most, cuts=(), kind=jnp.bfloat16):
    drawn = jax.random.normal(own_key, dims, jnp.float32) * spread
    if len(cuts) > 0:
        drawn = steps_of(own_key, dims, cuts, -0.22, 0.18) * drawn
    return jnp.clip(drawn, min=-most, max=most).astype(kind)


def noise_with(rng, shape, deviation, reach, pieces, heavy, held_as=jnp.bfloat16):
    entries = deviation * jax.random.normal(rng, shape, jnp.float32)
    if pieces:
        entries = entries * steps_of(rng, shape, pieces, -0.22, 0.18)
    return jnp.clip(raised(entries, jax.random.fold_in(rng, 3), *heavy), -reach, reach).astype(held_as)


def setup_inputs(seed: int = 0) -> dict:
    splits = jax.random.split(jax.random.key(seed), 15)
    return {
        "hidden_in": draw_hidden_in(jax.random.fold_in(splits[14], 71), 0),
        "lengths": draw_lengths(jax.random.fold_in(splits[14], 71), 0),
        "request_perm": jax.random.permutation(splits[2], R).astype(jnp.int32),
        "k_cache": draw_k_cache(jax.random.fold_in(splits[14], 71), 0),
        "v_cache": scatter_about(splits[4], (R, S_CAP, KVH * HD), 4.0, 16.0, ((1, 32), (2, 4))),
        "attn_gain": jnp.clip(1.0 + 0.1 * jax.random.normal(splits[5], (D,), jnp.float32), 0.5, 1.5).astype(jnp.bfloat16),
        "w_query": scatter_about(splits[6], (D, H * HD), D ** -0.5, 0.125, ((1, 4),)),
        "w_key": scatter_about(splits[7], (D, KVH * HD), (max(D // 256, 1)) ** -0.5, 2.0, ((1, 4),)),
        "w_value": scatter_about(splits[8], (D, KVH * HD), (D // 16) ** -0.5, 0.5, ((1, 4),)),
        "w_out": scatter_about(splits[9], (H * HD, D), (H * HD) ** -0.5, 0.125, ((0, 4),)),
        "mlp_gain": jnp.clip(1.0 + 0.18 * jax.random.normal(splits[10], (D,), jnp.float32), 0.099609375, 1.8984375).astype(jnp.bfloat16),
        "w_gate": scatter_about(splits[11], (FF, D), D ** -0.5, 0.125, ((0, 128),)),
        "w_up": scatter_about(splits[12], (FF, D), D ** -0.5, 0.125, ((0, 128),)),
        "w_down": noise_with(splits[13], (FF, D), (FF // 16) ** -0.5, 1.0, ((0, 128),), (0, 1, 128, 5.5)),
    }


norm_eps = 1e-05
rope_theta = 10000000.0
attn_scale = 0.015625
branch_scale = 0.5
neg_large = -1e+30

def rms_norm(values, gain_vector):
    floats = values.astype(jnp.float32)
    square_mean = lax.optimization_barrier(jnp.mean(floats * floats, axis=-1, keepdims=True))
    return (floats * lax.rsqrt(square_mean + norm_eps) * gain_vector.astype(jnp.float32)).astype(jnp.bfloat16)

def rotate(vectors, positions):
    half_size = vectors.shape[-1] // 2
    inverse = jnp.exp(jnp.arange(half_size, dtype=jnp.float32) * (-2.0 * math.log(rope_theta) / vectors.shape[-1]))
    angles = positions.astype(jnp.float32)[..., None] * inverse
    cosine = jnp.cos(angles)[..., None, :]
    sine = jnp.sin(angles)[..., None, :]
    first_half = vectors[..., :half_size]
    second_half = vectors[..., half_size:]
    return jnp.concatenate([first_half * cosine - second_half * sine, second_half * cosine + first_half * sine], axis=-1)

def reference(hidden_in, lengths, request_perm, k_cache, v_cache, attn_gain, w_query, w_key, w_value, w_out, mlp_gain, w_gate, w_up, w_down):
    row_total = STEPS * R
    group_size = H // KVH
    flat_in = hidden_in.reshape(row_total, D)
    normed = rms_norm(flat_in, attn_gain)
    positions = lengths[None, :] + jnp.arange(STEPS, dtype=jnp.int32)[:, None]
    query_raw = jnp.dot(normed, w_query, preferred_element_type=jnp.float32).reshape(STEPS, R, H, HD)
    key_raw = jnp.dot(normed, w_key, preferred_element_type=jnp.float32).reshape(STEPS, R, KVH, HD)
    value_new = jnp.dot(normed, w_value, preferred_element_type=jnp.float32).astype(jnp.bfloat16).reshape(STEPS, R, KVH * HD)
    queries = rotate(query_raw, positions).astype(jnp.bfloat16)
    key_new = rotate(key_raw, positions).astype(jnp.bfloat16).reshape(STEPS, R, KVH * HD)
    offsets = request_perm * S_CAP // R
    slot_ids = jnp.arange(S_CAP, dtype=jnp.int32)
    causal = jnp.arange(STEPS)[None, :] <= jnp.arange(STEPS)[:, None]

    def one_request(request_item):
        query_one, keys_one, values_one, new_keys, new_values, length_one, offset_one = request_item
        query_f = query_one.astype(jnp.float32).reshape(STEPS, KVH, group_size, HD)
        keys_f = keys_one.astype(jnp.float32).reshape(S_CAP, KVH, HD)
        values_f = values_one.astype(jnp.float32).reshape(S_CAP, KVH, HD)
        new_keys_f = new_keys.astype(jnp.float32).reshape(STEPS, KVH, HD)
        new_values_f = new_values.astype(jnp.float32).reshape(STEPS, KVH, HD)
        cache_live = (slot_ids - offset_one) % S_CAP < length_one
        cache_scores = jnp.einsum('tkgd,skd->kgts', query_f, keys_f, precision=lax.Precision.HIGHEST) * attn_scale
        new_scores = jnp.einsum('tkgd,ukd->kgtu', query_f, new_keys_f, precision=lax.Precision.HIGHEST) * attn_scale
        cache_scores = jnp.where(cache_live, cache_scores, neg_large)
        new_scores = jnp.where(causal, new_scores, neg_large)
        top_score = jnp.maximum(lax.optimization_barrier(jnp.max(cache_scores, axis=-1)), lax.optimization_barrier(jnp.max(new_scores, axis=-1)))
        cache_weights = jnp.where(cache_live, jnp.exp(cache_scores - top_score[..., None]), 0.0)
        new_weights = jnp.where(causal, jnp.exp(new_scores - top_score[..., None]), 0.0)
        weight_total = lax.optimization_barrier(jnp.sum(cache_weights, axis=-1)) + lax.optimization_barrier(jnp.sum(new_weights, axis=-1))
        cache_rounded = cache_weights.astype(jnp.bfloat16).astype(jnp.float32)
        new_rounded = new_weights.astype(jnp.bfloat16).astype(jnp.float32)
        mixed = jnp.einsum('kgts,skd->tkgd', cache_rounded, values_f, precision=lax.Precision.HIGHEST)
        mixed = mixed + jnp.einsum('kgtu,ukd->tkgd', new_rounded, new_values_f, precision=lax.Precision.HIGHEST)
        mixed = mixed / jnp.transpose(weight_total, (2, 0, 1))[..., None]
        return mixed.reshape(STEPS, H * HD)
    mapped = lax.map(one_request, (jnp.moveaxis(queries, 1, 0), k_cache, v_cache, jnp.moveaxis(key_new, 1, 0), jnp.moveaxis(value_new, 1, 0), lengths, offsets))
    heads = jnp.moveaxis(mapped, 1, 0).astype(jnp.bfloat16).reshape(row_total, H * HD)
    attended = jnp.dot(heads, w_out, preferred_element_type=jnp.float32)
    residual = (flat_in.astype(jnp.float32) + branch_scale * attended).astype(jnp.bfloat16)
    normed_mlp = rms_norm(residual, mlp_gain)
    contract_rows = (((1,), (1,)), ((), ()))
    gate = lax.dot_general(normed_mlp, w_gate, contract_rows, preferred_element_type=jnp.float32)
    up_proj = lax.dot_general(normed_mlp, w_up, contract_rows, preferred_element_type=jnp.float32)
    hidden = (jax.nn.silu(gate) * up_proj).astype(jnp.bfloat16)
    feed_forward = jnp.dot(hidden, w_down, preferred_element_type=jnp.float32)
    hidden_out = (residual.astype(jnp.float32) + branch_scale * feed_forward).astype(jnp.bfloat16).reshape(STEPS, R, D)
    return (hidden_out, key_new, value_new)
```

```python
import math

import jax
import jax.numpy as jnp
from jax import lax
from jax.sharding import PartitionSpec as P

H = 32
KVH = 8
HD = 64
S_CAP = 16384


norm_eps = 1e-05
rope_theta = 10000000.0
attn_scale = 0.015625
branch_scale = 0.5
neg_large = -1e30

CORE = ("seq", 1, 2)
ZAX = ("seq", 2, 4)
XAX = ("seq", 8, 4)
YAX = ("tp", 1, 4)
AXIS_SIZE = {"seq": 32, "tp": 4}


def coord(level):
    axis, stride, size = level
    return (lax.axis_index(axis) // stride) % size


def shift_perm(level, d):
    axis, stride, size = level
    pairs = []
    for i in range(AXIS_SIZE[axis]):
        c = (i // stride) % size
        pairs.append((i, i + ((c + d) % size - c) * stride))
    return pairs


def shifted(x, level, d):
    return lax.ppermute(x, level[0], shift_perm(level, d))


def take(x, index):
    return lax.dynamic_index_in_dim(x, index, axis=0, keepdims=False)


def softmax_scatter(level, top, total, mixed):
    size = level[2]
    c = coord(level)
    parts = [(take(top, c), take(total, c), take(mixed, c))]
    for d in range(1, size):
        dest = (c + d) % size
        parts.append(shifted((take(top, dest), take(total, dest), take(mixed, dest)), level, d))
    top_all = parts[0][0]
    for p in parts[1:]:
        top_all = jnp.maximum(top_all, p[0])
    total_all = 0.0
    mixed_all = 0.0
    for p in parts:
        factor = jnp.exp(p[0] - top_all)
        total_all = total_all + p[1] * factor
        mixed_all = mixed_all + p[2] * factor[..., None]
    return top_all, total_all, mixed_all


def sum_scatter_abs(x, level):
    size = level[2]
    c = coord(level)
    acc = take(x, c)
    for d in range(1, size):
        acc = acc + shifted(take(x, (c + d) % size), level, d)
    return acc


def gather_rel(x, level):
    size = level[2]
    parts = [x] + [shifted(x, level, d) for d in range(1, size)]
    return jnp.stack(parts, axis=0)


def sum_scatter_rel(x, level):
    size = level[2]
    acc = x[0]
    for d in range(1, size):
        acc = acc + shifted(x[size - d], level, d)
    return acc


def rms_norm(values, gain_vector):
    floats = values.astype(jnp.float32)
    square_mean = jnp.mean(floats * floats, axis=-1, keepdims=True)
    return (floats * lax.rsqrt(square_mean + norm_eps) * gain_vector.astype(jnp.float32)).astype(
        jnp.bfloat16
    )


def rotate(vectors, positions):
    half_size = vectors.shape[-1] // 2
    inverse = jnp.exp(
        jnp.arange(half_size, dtype=jnp.float32) * (-2.0 * math.log(rope_theta) / vectors.shape[-1])
    )
    angles = positions.astype(jnp.float32)[..., None] * inverse
    cosine = jnp.cos(angles)[..., None, :]
    sine = jnp.sin(angles)[..., None, :]
    first_half = vectors[..., :half_size]
    second_half = vectors[..., half_size:]
    return jnp.concatenate(
        [first_half * cosine - second_half * sine, second_half * cosine + first_half * sine],
        axis=-1,
    )


def attend_shard(query_sel, keys_sel, values_sel, lengths_sel, offsets_sel, slot_base):
    shard_len = keys_sel.shape[1]
    slot_ids = slot_base + jnp.arange(shard_len, dtype=jnp.int32)
    live = (slot_ids[None, :] - offsets_sel[:, None]) % S_CAP < lengths_sel[:, None]
    live_full = live[:, None, None, None, :]
    scores = (
        jnp.einsum("trkgd,rskd->rktgs", query_sel, keys_sel, preferred_element_type=jnp.float32)
        * attn_scale
    )
    top_part = jnp.max(jnp.where(live_full, scores, neg_large), axis=-1)
    weights = jnp.where(live_full, jnp.exp(scores - top_part[..., None]), 0.0)
    total_part = jnp.sum(weights, axis=-1)
    weights_rounded = weights.astype(jnp.bfloat16)
    mixed_part = jnp.einsum(
        "rktgs,rskd->rktgd", weights_rounded, values_sel, preferred_element_type=jnp.float32
    )
    return (top_part, total_part, mixed_part)


def local(
    hidden_in,
    lengths,
    request_perm,
    k_cache,
    v_cache,
    attn_gain,
    w_query,
    w_key,
    w_value,
    w_out,
    mlp_gain,
    w_gate,
    w_up,
    w_down,
):
    step_count, request_count, model_width = hidden_in.shape
    row_total = step_count * request_count
    group_size = H // KVH
    local_kv = k_cache.shape[2] // HD
    local_heads = local_kv * group_size
    shard_len = k_cache.shape[1]
    flat_in = hidden_in.reshape(row_total, model_width)
    normed = rms_norm(flat_in, attn_gain)
    positions = lengths[None, :] + jnp.arange(step_count, dtype=jnp.int32)[:, None]
    query_raw = jnp.dot(normed, w_query, preferred_element_type=jnp.float32).reshape(
        step_count, request_count, local_heads, HD
    )
    key_raw = jnp.dot(normed, w_key, preferred_element_type=jnp.float32).reshape(
        step_count, request_count, local_kv, HD
    )
    value_new = (
        jnp.dot(normed, w_value, preferred_element_type=jnp.float32)
        .astype(jnp.bfloat16)
        .reshape(step_count, request_count, local_kv, HD)
    )
    queries = (
        rotate(query_raw, positions)
        .astype(jnp.bfloat16)
        .reshape(step_count, request_count, local_kv, group_size, HD)
    )
    key_new = rotate(key_raw, positions).astype(jnp.bfloat16)
    offsets = request_perm * S_CAP // request_count
    slot_base = lax.axis_index("seq") * shard_len
    cache_keys = k_cache.reshape(request_count, shard_len, local_kv, HD)
    cache_values = v_cache.reshape(request_count, shard_len, local_kv, HD)
    top_part, total_part, mixed_part = attend_shard(
        queries, cache_keys, cache_values, lengths, offsets, slot_base
    )

    levels = (CORE, ZAX, XAX)
    top_s = top_part.reshape((2, 4, 4, -1) + top_part.shape[1:])
    total_s = total_part.reshape((2, 4, 4, -1) + total_part.shape[1:])
    mixed_s = mixed_part.reshape((2, 4, 4, -1) + mixed_part.shape[1:])
    for level in levels:
        top_s, total_s, mixed_s = softmax_scatter(level, top_s, total_s, mixed_s)
    own_count = top_s.shape[0]
    first_req = ((coord(CORE) * 4 + coord(ZAX)) * 4 + coord(XAX)) * own_count

    def own(x):
        return lax.dynamic_slice_in_dim(x, first_req, own_count, axis=1)

    queries_own = own(queries)
    key_own = own(key_new)
    value_own = own(value_new)
    causal = jnp.arange(step_count)[None, :] <= jnp.arange(step_count)[:, None]
    causal_full = causal[None, None, :, None, :]
    new_scores = (
        jnp.einsum("trkgd,urkd->rktgu", queries_own, key_own, preferred_element_type=jnp.float32)
        * attn_scale
    )
    top_new = jnp.max(jnp.where(causal_full, new_scores, neg_large), axis=-1)
    top_final = jnp.maximum(top_s, top_new)
    new_weights = jnp.where(causal_full, jnp.exp(new_scores - top_final[..., None]), 0.0)
    new_mixed = jnp.einsum(
        "rktgu,urkd->rktgd",
        new_weights.astype(jnp.bfloat16),
        value_own,
        preferred_element_type=jnp.float32,
    )
    weight_cache = jnp.exp(top_s - top_final)
    denominator = total_s * weight_cache + jnp.sum(new_weights, axis=-1)
    heads = (mixed_s * weight_cache[..., None] + new_mixed) / denominator[..., None]
    heads = (
        jnp.transpose(heads, (2, 0, 1, 3, 4))
        .reshape(step_count * own_count, local_heads * HD)
        .astype(jnp.bfloat16)
    )
    attended_part = jnp.dot(heads, w_out, preferred_element_type=jnp.float32).reshape(
        step_count, own_count, model_width
    )
    attended = sum_scatter_abs(attended_part, YAX)
    step_own = coord(YAX)
    hidden_own = lax.dynamic_slice_in_dim(take(hidden_in, step_own), first_req, own_count, axis=0)
    residual = (hidden_own.astype(jnp.float32) + branch_scale * attended).astype(jnp.bfloat16)
    normed_mlp = rms_norm(residual, mlp_gain)

    gather_levels = (YAX, XAX, ZAX, CORE)
    rows = normed_mlp
    for level in gather_levels:
        rows = gather_rel(rows, level)
    block_shape = rows.shape[:-1]
    rows = rows.reshape(-1, model_width)
    contract_rows = (((1,), (1,)), ((), ()))
    gate = lax.dot_general(rows, w_gate, contract_rows, preferred_element_type=jnp.float32)
    up_proj = lax.dot_general(rows, w_up, contract_rows, preferred_element_type=jnp.float32)
    hidden = (jax.nn.silu(gate) * up_proj).astype(jnp.bfloat16)
    feed_forward = jnp.dot(hidden, w_down, preferred_element_type=jnp.float32).reshape(
        block_shape + (model_width,)
    )
    for level in reversed(gather_levels):
        feed_forward = sum_scatter_rel(feed_forward, level)
    output = (residual.astype(jnp.float32) + branch_scale * feed_forward).astype(jnp.bfloat16)

    out_rows = output
    for level in gather_levels:
        out_rows = gather_rel(out_rows, level)
    for axis_pos, level in enumerate((CORE, ZAX, XAX, YAX)):
        size = level[2]
        order = (coord(level) - jnp.arange(size)) % size
        out_rows = jnp.take(out_rows, order, axis=axis_pos)
    hidden_out = jnp.transpose(out_rows, (3, 0, 1, 2, 4, 5)).reshape(
        step_count, request_count, model_width
    )
    key_out = key_new.reshape(step_count, request_count, local_kv * HD)
    value_out = value_new.reshape(step_count, request_count, local_kv * HD)
    return (hidden_out, key_out, value_out)


def solution(mesh):
    placed = (
        P(),
        P(),
        P(),
        P(None, "seq", "tp"),
        P(None, "seq", "tp"),
        P(),
        P(None, "tp"),
        P(None, "tp"),
        P(None, "tp"),
        P("tp", None),
        P(),
        P(("seq", "tp"), None),
        P(("seq", "tp"), None),
        P(("seq", "tp"), None),
    )
    return jax.shard_map(
        local,
        mesh=mesh,
        in_specs=placed,
        out_specs=(P(), P(None, None, "tp"), P(None, None, "tp")),
        check_vma=False,
    )
```

```python
import math

import jax
import jax.numpy as jnp
from jax import lax
from jax.sharding import PartitionSpec as P

H = 32
KVH = 8
HD = 64
S_CAP = 16384


norm_eps = 1e-05
rope_theta = 10000000.0
attn_scale = 0.015625
branch_scale = 0.5
neg_large = -1e30

CORE = ("seq", 1, 2)
ZAX = ("seq", 2, 4)
XAX = ("seq", 8, 4)
YAX = ("tp", 1, 4)
AXIS_SIZE = {"seq": 32, "tp": 4}


def coord(level):
    axis, stride, size = level
    return (lax.axis_index(axis) // stride) % size


def shift_perm(level, d):
    axis, stride, size = level
    pairs = []
    for i in range(AXIS_SIZE[axis]):
        c = (i // stride) % size
        pairs.append((i, i + ((c + d) % size - c) * stride))
    return pairs


def shifted(x, level, d):
    return lax.ppermute(x, level[0], shift_perm(level, d))


def take(x, index):
    return lax.dynamic_index_in_dim(x, index, axis=0, keepdims=False)


def softmax_scatter(level, top, total, mixed):
    size = level[2]
    c = coord(level)
    parts = [(take(top, c), take(total, c), take(mixed, c))]
    for d in range(1, size):
        dest = (c + d) % size
        parts.append(shifted((take(top, dest), take(total, dest), take(mixed, dest)), level, d))
    top_all = parts[0][0]
    for p in parts[1:]:
        top_all = jnp.maximum(top_all, p[0])
    total_all = 0.0
    mixed_all = 0.0
    for p in parts:
        factor = jnp.exp(p[0] - top_all)
        total_all = total_all + p[1] * factor
        mixed_all = mixed_all + p[2] * factor[..., None]
    return top_all, total_all, mixed_all


def sum_scatter_abs(x, level):
    size = level[2]
    c = coord(level)
    acc = take(x, c)
    for d in range(1, size):
        acc = acc + shifted(take(x, (c + d) % size), level, d)
    return acc


def gather_rel(x, level):
    size = level[2]
    parts = [x] + [shifted(x, level, d) for d in range(1, size)]
    return jnp.stack(parts, axis=0)


def sum_scatter_rel(x, level):
    size = level[2]
    acc = x[0]
    for d in range(1, size):
        acc = acc + shifted(x[size - d], level, d)
    return acc


def rms_norm(values, gain_vector):
    floats = values.astype(jnp.float32)
    square_mean = jnp.mean(floats * floats, axis=-1, keepdims=True)
    return (floats * lax.rsqrt(square_mean + norm_eps) * gain_vector.astype(jnp.float32)).astype(
        jnp.bfloat16
    )


def rotate(vectors, positions):
    half_size = vectors.shape[-1] // 2
    inverse = jnp.exp(
        jnp.arange(half_size, dtype=jnp.float32) * (-2.0 * math.log(rope_theta) / vectors.shape[-1])
    )
    angles = positions.astype(jnp.float32)[..., None] * inverse
    cosine = jnp.cos(angles)[..., None, :]
    sine = jnp.sin(angles)[..., None, :]
    first_half = vectors[..., :half_size]
    second_half = vectors[..., half_size:]
    return jnp.concatenate(
        [first_half * cosine - second_half * sine, second_half * cosine + first_half * sine],
        axis=-1,
    )


def attend_shard(query_sel, keys_sel, values_sel, lengths_sel, offsets_sel, slot_base):
    step_count, request_count, local_kv, group_size, head_dim = query_sel.shape
    shard_len = keys_sel.shape[1]
    slot_ids = slot_base + jnp.arange(shard_len, dtype=jnp.int32)
    live = (slot_ids[None, :] - offsets_sel[:, None]) % S_CAP < lengths_sel[:, None]
    live_full = live[:, None, :]
    same_head = jnp.eye(local_kv, dtype=jnp.bool_)
    query_rows = jnp.transpose(query_sel, (1, 2, 0, 3, 4))
    spread = jnp.where(
        same_head[None, :, None, None, :, None],
        query_rows[:, :, :, :, None, :],
        jnp.zeros((), query_sel.dtype),
    ).reshape(request_count, local_kv * step_count * group_size, local_kv * head_dim)
    scores = (
        jnp.einsum("rqc,rsc->rqs", spread, keys_sel, preferred_element_type=jnp.float32)
        * attn_scale
    )
    top_part = jnp.max(jnp.where(live_full, scores, neg_large), axis=-1)
    weights = jnp.where(live_full, jnp.exp(scores - top_part[..., None]), 0.0)
    total_part = jnp.sum(weights, axis=-1)
    weights_rounded = weights.astype(jnp.bfloat16)
    mixed_wide = jnp.einsum(
        "rqs,rsc->rqc", weights_rounded, values_sel, preferred_element_type=jnp.float32
    ).reshape(request_count, local_kv, step_count, group_size, local_kv, head_dim)
    mixed_part = jnp.sum(
        jnp.where(same_head[None, :, None, None, :, None], mixed_wide, 0.0), axis=4
    )
    shape = (request_count, local_kv, step_count, group_size)
    return (top_part.reshape(shape), total_part.reshape(shape), mixed_part)


def local(
    hidden_in,
    lengths,
    request_perm,
    k_cache,
    v_cache,
    attn_gain,
    w_query,
    w_key,
    w_value,
    w_out,
    mlp_gain,
    w_gate,
    w_up,
    w_down,
):
    step_count, request_count, model_width = hidden_in.shape
    row_total = step_count * request_count
    group_size = H // KVH
    local_kv = k_cache.shape[2] // HD
    local_heads = local_kv * group_size
    shard_len = k_cache.shape[1]
    flat_in = hidden_in.reshape(row_total, model_width)
    normed = rms_norm(flat_in, attn_gain)
    positions = lengths[None, :] + jnp.arange(step_count, dtype=jnp.int32)[:, None]
    query_raw = jnp.dot(normed, w_query, preferred_element_type=jnp.float32).reshape(
        step_count, request_count, local_heads, HD
    )
    key_raw = jnp.dot(normed, w_key, preferred_element_type=jnp.float32).reshape(
        step_count, request_count, local_kv, HD
    )
    value_new = (
        jnp.dot(normed, w_value, preferred_element_type=jnp.float32)
        .astype(jnp.bfloat16)
        .reshape(step_count, request_count, local_kv, HD)
    )
    queries = (
        rotate(query_raw, positions)
        .astype(jnp.bfloat16)
        .reshape(step_count, request_count, local_kv, group_size, HD)
    )
    key_new = rotate(key_raw, positions).astype(jnp.bfloat16)
    offsets = request_perm * S_CAP // request_count
    slot_base = lax.axis_index("seq") * shard_len
    top_part, total_part, mixed_part = attend_shard(
        queries, k_cache, v_cache, lengths, offsets, slot_base
    )

    levels = (CORE, ZAX, XAX)
    top_s = top_part.reshape((2, 4, 4, -1) + top_part.shape[1:])
    total_s = total_part.reshape((2, 4, 4, -1) + total_part.shape[1:])
    mixed_s = mixed_part.reshape((2, 4, 4, -1) + mixed_part.shape[1:])
    for level in levels:
        top_s, total_s, mixed_s = softmax_scatter(level, top_s, total_s, mixed_s)
    own_count = top_s.shape[0]
    first_req = ((coord(CORE) * 4 + coord(ZAX)) * 4 + coord(XAX)) * own_count

    def own(x):
        return lax.dynamic_slice_in_dim(x, first_req, own_count, axis=1)

    queries_own = own(queries)
    key_own = own(key_new)
    value_own = own(value_new)
    causal = jnp.arange(step_count)[None, :] <= jnp.arange(step_count)[:, None]
    causal_full = causal[None, None, :, None, :]
    new_scores = (
        jnp.einsum("trkgd,urkd->rktgu", queries_own, key_own, preferred_element_type=jnp.float32)
        * attn_scale
    )
    top_new = jnp.max(jnp.where(causal_full, new_scores, neg_large), axis=-1)
    top_final = jnp.maximum(top_s, top_new)
    new_weights = jnp.where(causal_full, jnp.exp(new_scores - top_final[..., None]), 0.0)
    new_mixed = jnp.einsum(
        "rktgu,urkd->rktgd",
        new_weights.astype(jnp.bfloat16),
        value_own,
        preferred_element_type=jnp.float32,
    )
    weight_cache = jnp.exp(top_s - top_final)
    denominator = total_s * weight_cache + jnp.sum(new_weights, axis=-1)
    heads = (mixed_s * weight_cache[..., None] + new_mixed) / denominator[..., None]
    heads = (
        jnp.transpose(heads, (2, 0, 1, 3, 4))
        .reshape(step_count * own_count, local_heads * HD)
        .astype(jnp.bfloat16)
    )
    attended_part = jnp.dot(heads, w_out, preferred_element_type=jnp.float32).reshape(
        step_count, own_count, model_width
    )
    attended = sum_scatter_abs(attended_part, YAX)
    step_own = coord(YAX)
    hidden_own = lax.dynamic_slice_in_dim(take(hidden_in, step_own), first_req, own_count, axis=0)
    residual = (hidden_own.astype(jnp.float32) + branch_scale * attended).astype(jnp.bfloat16)
    normed_mlp = rms_norm(residual, mlp_gain)

    gather_levels = (YAX, XAX, ZAX, CORE)
    rows = normed_mlp
    for level in gather_levels:
        rows = gather_rel(rows, level)
    block_shape = rows.shape[:-1]
    rows = rows.reshape(-1, model_width)
    contract_rows = (((1,), (1,)), ((), ()))
    gate = lax.dot_general(rows, w_gate, contract_rows, preferred_element_type=jnp.float32)
    up_proj = lax.dot_general(rows, w_up, contract_rows, preferred_element_type=jnp.float32)
    hidden = (jax.nn.silu(gate) * up_proj).astype(jnp.bfloat16)
    feed_forward = jnp.dot(hidden, w_down, preferred_element_type=jnp.float32).reshape(
        block_shape + (model_width,)
    )
    for level in reversed(gather_levels):
        feed_forward = sum_scatter_rel(feed_forward, level)
    output = (residual.astype(jnp.float32) + branch_scale * feed_forward).astype(jnp.bfloat16)

    out_rows = output
    for level in gather_levels:
        out_rows = gather_rel(out_rows, level)
    order_levels = (YAX, CORE, ZAX, XAX)
    block_rows = out_rows.shape[4]
    blocks = out_rows.reshape(-1, block_rows * model_width)
    dest = jnp.arange(blocks.shape[0], dtype=jnp.int32)
    member = {}
    for level in reversed(order_levels):
        member[level] = dest % level[2]
        dest = dest // level[2]
    source = jnp.zeros_like(dest)
    for level in (CORE, ZAX, XAX, YAX):
        size = level[2]
        source = source * size + (coord(level) - member[level]) % size
    one_hot = (source[:, None] == jnp.arange(blocks.shape[0], dtype=jnp.int32)[None, :]).astype(
        blocks.dtype
    )
    hidden_out = (
        jnp.dot(one_hot, blocks, preferred_element_type=jnp.float32)
        .astype(jnp.bfloat16)
        .reshape(step_count, request_count, model_width)
    )
    key_out = key_new.reshape(step_count, request_count, local_kv * HD)
    value_out = value_new.reshape(step_count, request_count, local_kv * HD)
    return (hidden_out, key_out, value_out)


def solution(mesh):
    placed = (
        P(),
        P(),
        P(),
        P(None, "seq", "tp"),
        P(None, "seq", "tp"),
        P(),
        P(None, "tp"),
        P(None, "tp"),
        P(None, "tp"),
        P("tp", None),
        P(),
        P(("seq", "tp"), None),
        P(("seq", "tp"), None),
        P(("seq", "tp"), None),
    )
    return jax.shard_map(
        local,
        mesh=mesh,
        in_specs=placed,
        out_specs=(P(), P(None, None, "tp"), P(None, None, "tp")),
        check_vma=False,
    )
```

```python
import math

import jax
import jax.numpy as jnp
from jax import lax
from jax.experimental import pallas as pl
from jax.experimental.pallas import tpu as pltpu
from jax.sharding import PartitionSpec as P

H = 32
KVH = 8
HD = 64
S_CAP = 16384


norm_eps = 1e-05
rope_theta = 10000000.0
attn_scale = 0.015625
branch_scale = 0.5
neg_large = -1e30

CORE = ("seq", 1, 2)
ZAX = ("seq", 2, 4)
XAX = ("seq", 8, 4)
YAX = ("tp", 1, 4)
AXIS_SIZE = {"seq": 32, "tp": 4}


def coord(level):
    axis, stride, size = level
    return (lax.axis_index(axis) // stride) % size


def shift_perm(level, d):
    axis, stride, size = level
    pairs = []
    for i in range(AXIS_SIZE[axis]):
        c = (i // stride) % size
        pairs.append((i, i + ((c + d) % size - c) * stride))
    return pairs


def shifted(x, level, d):
    return lax.ppermute(x, level[0], shift_perm(level, d))


def take(x, index):
    return lax.dynamic_index_in_dim(x, index, axis=0, keepdims=False)


def softmax_scatter(level, top, total, mixed):
    size = level[2]
    c = coord(level)
    parts = [(take(top, c), take(total, c), take(mixed, c))]
    for d in range(1, size):
        dest = (c + d) % size
        parts.append(shifted((take(top, dest), take(total, dest), take(mixed, dest)), level, d))
    top_all = parts[0][0]
    for p in parts[1:]:
        top_all = jnp.maximum(top_all, p[0])
    total_all = 0.0
    mixed_all = 0.0
    for p in parts:
        factor = jnp.exp(p[0] - top_all)
        total_all = total_all + p[1] * factor
        mixed_all = mixed_all + p[2] * factor[..., None]
    return top_all, total_all, mixed_all


def sum_scatter_abs(x, level):
    size = level[2]
    c = coord(level)
    acc = take(x, c)
    for d in range(1, size):
        acc = acc + shifted(take(x, (c + d) % size), level, d)
    return acc


def gather_rel(x, level):
    size = level[2]
    parts = [x] + [shifted(x, level, d) for d in range(1, size)]
    return jnp.stack(parts, axis=0)


def sum_scatter_rel(x, level):
    size = level[2]
    acc = x[0]
    for d in range(1, size):
        acc = acc + shifted(x[size - d], level, d)
    return acc


def rms_norm(values, gain_vector):
    floats = values.astype(jnp.float32)
    square_mean = jnp.mean(floats * floats, axis=-1, keepdims=True)
    return (floats * lax.rsqrt(square_mean + norm_eps) * gain_vector.astype(jnp.float32)).astype(
        jnp.bfloat16
    )


def rotate(vectors, positions):
    half_size = vectors.shape[-1] // 2
    inverse = jnp.exp(
        jnp.arange(half_size, dtype=jnp.float32) * (-2.0 * math.log(rope_theta) / vectors.shape[-1])
    )
    angles = positions.astype(jnp.float32)[..., None] * inverse
    cosine = jnp.cos(angles)[..., None, :]
    sine = jnp.sin(angles)[..., None, :]
    first_half = vectors[..., :half_size]
    second_half = vectors[..., half_size:]
    return jnp.concatenate(
        [first_half * cosine - second_half * sine, second_half * cosine + first_half * sine],
        axis=-1,
    )


BLOCK_REQ = 8


def cache_kernel(start_ref, len_ref, q_ref, k_ref, v_ref, top_ref, total_ref, mixed_ref):
    block = pl.program_id(0)
    rows = q_ref.shape[1]
    half = rows // 2
    head_dim = mixed_ref.shape[2]
    shard_len = k_ref.shape[1]
    slots = lax.broadcasted_iota(jnp.int32, (1, shard_len), 1)
    for i in range(q_ref.shape[0]):
        r = block * q_ref.shape[0] + i
        rel = slots + start_ref[r]
        rel = jnp.where(rel >= S_CAP, rel - S_CAP, rel)
        live = rel < len_ref[r]
        scores = lax.dot_general(q_ref[i], k_ref[i], (((1,), (1,)), ((), ())),
                                 preferred_element_type=jnp.float32) * attn_scale
        top = jnp.max(jnp.where(live, scores, neg_large), axis=-1, keepdims=True)
        weights = jnp.where(live, jnp.exp(scores - top), 0.0)
        top_ref[i] = top
        total_ref[i] = jnp.sum(weights, axis=-1, keepdims=True)
        mixed = jnp.dot(weights.astype(jnp.bfloat16), v_ref[i], preferred_element_type=jnp.float32)
        mixed_ref[i, 0:half, :] = mixed[0:half, 0:head_dim]
        mixed_ref[i, half:rows, :] = mixed[half:rows, head_dim:2 * head_dim]


def cache_attention(start, lengths, spread, keys, values, head_dim):
    req, rows, width = spread.shape
    shard_len = keys.shape[1]
    grid = (req // BLOCK_REQ,)
    def blk(b, s, l):
        return (b, 0, 0)
    return pl.pallas_call(
        cache_kernel,
        out_shape=(jax.ShapeDtypeStruct((req, rows, 1), jnp.float32),
                   jax.ShapeDtypeStruct((req, rows, 1), jnp.float32),
                   jax.ShapeDtypeStruct((req, rows, head_dim), jnp.float32)),
        grid_spec=pltpu.PrefetchScalarGridSpec(
            num_scalar_prefetch=2, grid=grid,
            in_specs=[pl.BlockSpec((BLOCK_REQ, rows, width), blk),
                      pl.BlockSpec((BLOCK_REQ, shard_len, width), blk),
                      pl.BlockSpec((BLOCK_REQ, shard_len, width), blk)],
            out_specs=[pl.BlockSpec((BLOCK_REQ, rows, 1), blk),
                       pl.BlockSpec((BLOCK_REQ, rows, 1), blk),
                       pl.BlockSpec((BLOCK_REQ, rows, head_dim), blk)]),
    )(start, lengths, spread, keys, values)


def attend_shard(query_sel, keys_sel, values_sel, lengths_sel, offsets_sel, slot_base):
    step_count, request_count, local_kv, group_size, head_dim = query_sel.shape
    query_rows = jnp.transpose(query_sel, (1, 2, 0, 3, 4)).reshape(
        request_count, local_kv, step_count * group_size, head_dim
    )
    blank = jnp.zeros((request_count, step_count * group_size, head_dim), query_sel.dtype)
    spread = jnp.concatenate(
        [
            jnp.concatenate([query_rows[:, k] if j == k else blank for j in range(local_kv)], axis=-1)
            for k in range(local_kv)
        ],
        axis=1,
    )
    start = (slot_base - offsets_sel) % S_CAP
    top_part, total_part, mixed_part = cache_attention(
        start, lengths_sel, spread, keys_sel, values_sel, head_dim
    )
    shape = (request_count, local_kv, step_count, group_size)
    return (top_part.reshape(shape), total_part.reshape(shape), mixed_part.reshape(shape + (head_dim,)))


def local(
    hidden_in,
    lengths,
    request_perm,
    k_cache,
    v_cache,
    attn_gain,
    w_query,
    w_key,
    w_value,
    w_out,
    mlp_gain,
    w_gate,
    w_up,
    w_down,
):
    step_count, request_count, model_width = hidden_in.shape
    row_total = step_count * request_count
    group_size = H // KVH
    local_kv = k_cache.shape[2] // HD
    local_heads = local_kv * group_size
    shard_len = k_cache.shape[1]
    flat_in = hidden_in.reshape(row_total, model_width)
    normed = rms_norm(flat_in, attn_gain)
    positions = lengths[None, :] + jnp.arange(step_count, dtype=jnp.int32)[:, None]
    query_raw = jnp.dot(normed, w_query, preferred_element_type=jnp.float32).reshape(
        step_count, request_count, local_heads, HD
    )
    key_raw = jnp.dot(normed, w_key, preferred_element_type=jnp.float32).reshape(
        step_count, request_count, local_kv, HD
    )
    value_new = (
        jnp.dot(normed, w_value, preferred_element_type=jnp.float32)
        .astype(jnp.bfloat16)
        .reshape(step_count, request_count, local_kv, HD)
    )
    queries = (
        rotate(query_raw, positions)
        .astype(jnp.bfloat16)
        .reshape(step_count, request_count, local_kv, group_size, HD)
    )
    key_new = rotate(key_raw, positions).astype(jnp.bfloat16)
    offsets = request_perm * S_CAP // request_count
    slot_base = lax.axis_index("seq") * shard_len
    top_part, total_part, mixed_part = attend_shard(
        queries, k_cache, v_cache, lengths, offsets, slot_base
    )

    levels = (CORE, ZAX, XAX)
    top_s = top_part.reshape((2, 4, 4, -1) + top_part.shape[1:])
    total_s = total_part.reshape((2, 4, 4, -1) + total_part.shape[1:])
    mixed_s = mixed_part.reshape((2, 4, 4, -1) + mixed_part.shape[1:])
    for level in levels:
        top_s, total_s, mixed_s = softmax_scatter(level, top_s, total_s, mixed_s)
    own_count = top_s.shape[0]
    first_req = ((coord(CORE) * 4 + coord(ZAX)) * 4 + coord(XAX)) * own_count

    def own(x):
        return lax.dynamic_slice_in_dim(x, first_req, own_count, axis=1)

    queries_own = own(queries)
    key_own = own(key_new)
    value_own = own(value_new)
    causal = jnp.arange(step_count)[None, :] <= jnp.arange(step_count)[:, None]
    causal_full = causal[None, None, :, None, :]
    new_scores = (
        jnp.einsum("trkgd,urkd->rktgu", queries_own, key_own, preferred_element_type=jnp.float32)
        * attn_scale
    )
    top_new = jnp.max(jnp.where(causal_full, new_scores, neg_large), axis=-1)
    top_final = jnp.maximum(top_s, top_new)
    new_weights = jnp.where(causal_full, jnp.exp(new_scores - top_final[..., None]), 0.0)
    new_mixed = jnp.einsum(
        "rktgu,urkd->rktgd",
        new_weights.astype(jnp.bfloat16),
        value_own,
        preferred_element_type=jnp.float32,
    )
    weight_cache = jnp.exp(top_s - top_final)
    denominator = total_s * weight_cache + jnp.sum(new_weights, axis=-1)
    heads = (mixed_s * weight_cache[..., None] + new_mixed) / denominator[..., None]
    heads = (
        jnp.transpose(heads, (2, 0, 1, 3, 4))
        .reshape(step_count * own_count, local_heads * HD)
        .astype(jnp.bfloat16)
    )
    attended_part = jnp.dot(heads, w_out, preferred_element_type=jnp.float32).reshape(
        step_count, own_count, model_width
    )
    attended = sum_scatter_abs(attended_part, YAX)
    step_own = coord(YAX)
    hidden_own = lax.dynamic_slice_in_dim(take(hidden_in, step_own), first_req, own_count, axis=0)
    residual = (hidden_own.astype(jnp.float32) + branch_scale * attended).astype(jnp.bfloat16)
    normed_mlp = rms_norm(residual, mlp_gain)

    gather_levels = (YAX, XAX, ZAX, CORE)
    rows = normed_mlp
    for level in gather_levels:
        rows = gather_rel(rows, level)
    block_shape = rows.shape[:-1]
    rows = rows.reshape(-1, model_width)
    contract_rows = (((1,), (1,)), ((), ()))
    gate = lax.dot_general(rows, w_gate, contract_rows, preferred_element_type=jnp.float32)
    up_proj = lax.dot_general(rows, w_up, contract_rows, preferred_element_type=jnp.float32)
    hidden = (jax.nn.silu(gate) * up_proj).astype(jnp.bfloat16)
    feed_forward = jnp.dot(hidden, w_down, preferred_element_type=jnp.float32).reshape(
        block_shape + (model_width,)
    )
    for level in reversed(gather_levels):
        feed_forward = sum_scatter_rel(feed_forward, level)
    output = (residual.astype(jnp.float32) + branch_scale * feed_forward).astype(jnp.bfloat16)

    out_rows = output
    for level in gather_levels:
        out_rows = gather_rel(out_rows, level)
    order_levels = (YAX, CORE, ZAX, XAX)
    block_rows = out_rows.shape[4]
    blocks = out_rows.reshape(-1, block_rows * model_width)
    dest = jnp.arange(blocks.shape[0], dtype=jnp.int32)
    member = {}
    for level in reversed(order_levels):
        member[level] = dest % level[2]
        dest = dest // level[2]
    source = jnp.zeros_like(dest)
    for level in (CORE, ZAX, XAX, YAX):
        size = level[2]
        source = source * size + (coord(level) - member[level]) % size
    one_hot = (source[:, None] == jnp.arange(blocks.shape[0], dtype=jnp.int32)[None, :]).astype(
        blocks.dtype
    )
    hidden_out = (
        jnp.dot(one_hot, blocks, preferred_element_type=jnp.float32)
        .astype(jnp.bfloat16)
        .reshape(step_count, request_count, model_width)
    )
    key_out = key_new.reshape(step_count, request_count, local_kv * HD)
    value_out = value_new.reshape(step_count, request_count, local_kv * HD)
    return (hidden_out, key_out, value_out)


def solution(mesh):
    placed = (
        P(),
        P(),
        P(),
        P(None, "seq", "tp"),
        P(None, "seq", "tp"),
        P(),
        P(None, "tp"),
        P(None, "tp"),
        P(None, "tp"),
        P("tp", None),
        P(),
        P(("seq", "tp"), None),
        P(("seq", "tp"), None),
        P(("seq", "tp"), None),
    )
    return jax.shard_map(
        local,
        mesh=mesh,
        in_specs=placed,
        out_specs=(P(), P(None, None, "tp"), P(None, None, "tp")),
        check_vma=False,
    )
```

```python
import math

import jax
import jax.numpy as jnp
from jax import lax
from jax.experimental import pallas as pl
from jax.experimental.pallas import tpu as pltpu
from jax.sharding import PartitionSpec as P

H = 32
KVH = 8
HD = 64
S_CAP = 16384


norm_eps = 1e-05
rope_theta = 10000000.0
attn_scale = 0.015625
branch_scale = 0.5
neg_large = -1e30

CORE = ("seq", 1, 2)
ZAX = ("seq", 2, 4)
XAX = ("seq", 8, 4)
YAX = ("tp", 1, 4)
AXIS_SIZE = {"seq": 32, "tp": 4}


def coord(level):
    axis, stride, size = level
    return (lax.axis_index(axis) // stride) % size


def shift_perm(level, d):
    axis, stride, size = level
    pairs = []
    for i in range(AXIS_SIZE[axis]):
        c = (i // stride) % size
        pairs.append((i, i + ((c + d) % size - c) * stride))
    return pairs


def shifted(x, level, d):
    return lax.ppermute(x, level[0], shift_perm(level, d))


def take(x, index):
    return lax.dynamic_index_in_dim(x, index, axis=0, keepdims=False)


def softmax_scatter(level, packed):
    size = level[2]
    c = coord(level)
    parts = [take(packed, c)]
    for d in range(1, size):
        parts.append(shifted(take(packed, (c + d) % size), level, d))
    head_dim = packed.shape[-1] - 2
    top_all = parts[0][..., head_dim]
    for p in parts[1:]:
        top_all = jnp.maximum(top_all, p[..., head_dim])
    total_all = 0.0
    mixed_all = 0.0
    for p in parts:
        factor = jnp.exp(p[..., head_dim] - top_all)
        total_all = total_all + p[..., head_dim + 1] * factor
        mixed_all = mixed_all + p[..., :head_dim] * factor[..., None]
    return jnp.concatenate([mixed_all, top_all[..., None], total_all[..., None]], axis=-1)


def sum_scatter_abs(x, level):
    size = level[2]
    c = coord(level)
    acc = take(x, c)
    for d in range(1, size):
        acc = acc + shifted(take(x, (c + d) % size), level, d)
    return acc


def gather_rel(x, level):
    size = level[2]
    parts = [x] + [shifted(x, level, d) for d in range(1, size)]
    return jnp.stack(parts, axis=0)


def sum_scatter_rel(x, level):
    size = level[2]
    acc = x[0]
    for d in range(1, size):
        acc = acc + shifted(x[size - d], level, d)
    return acc


def rms_norm(values, gain_vector):
    floats = values.astype(jnp.float32)
    square_mean = jnp.mean(floats * floats, axis=-1, keepdims=True)
    return (floats * lax.rsqrt(square_mean + norm_eps) * gain_vector.astype(jnp.float32)).astype(
        jnp.bfloat16
    )


def rotate(vectors, positions):
    half_size = vectors.shape[-1] // 2
    inverse = jnp.exp(
        jnp.arange(half_size, dtype=jnp.float32) * (-2.0 * math.log(rope_theta) / vectors.shape[-1])
    )
    angles = positions.astype(jnp.float32)[..., None] * inverse
    cosine = jnp.cos(angles)[..., None, :]
    sine = jnp.sin(angles)[..., None, :]
    first_half = vectors[..., :half_size]
    second_half = vectors[..., half_size:]
    return jnp.concatenate(
        [first_half * cosine - second_half * sine, second_half * cosine + first_half * sine],
        axis=-1,
    )


BLOCK_REQ = 8


def cache_kernel(start_ref, len_ref, q_ref, k_ref, v_ref, top_ref, total_ref, mixed_ref):
    block = pl.program_id(0)
    rows = q_ref.shape[1]
    half = rows // 2
    head_dim = mixed_ref.shape[2]
    shard_len = k_ref.shape[1]
    slots = lax.broadcasted_iota(jnp.int32, (1, shard_len), 1)
    for i in range(q_ref.shape[0]):
        r = block * q_ref.shape[0] + i
        rel = slots + start_ref[r]
        rel = jnp.where(rel >= S_CAP, rel - S_CAP, rel)
        live = rel < len_ref[r]
        scores = lax.dot_general(q_ref[i], k_ref[i], (((1,), (1,)), ((), ())),
                                 preferred_element_type=jnp.float32) * attn_scale
        top = jnp.max(jnp.where(live, scores, neg_large), axis=-1, keepdims=True)
        weights = jnp.where(live, jnp.exp(scores - top), 0.0)
        top_ref[i] = top
        total_ref[i] = jnp.sum(weights, axis=-1, keepdims=True)
        mixed = jnp.dot(weights.astype(jnp.bfloat16), v_ref[i], preferred_element_type=jnp.float32)
        mixed_ref[i, 0:half, :] = mixed[0:half, 0:head_dim]
        mixed_ref[i, half:rows, :] = mixed[half:rows, head_dim:2 * head_dim]


def cache_attention(start, lengths, spread, keys, values, head_dim):
    req, rows, width = spread.shape
    shard_len = keys.shape[1]
    grid = (req // BLOCK_REQ,)
    def blk(b, s, l):
        return (b, 0, 0)
    return pl.pallas_call(
        cache_kernel,
        out_shape=(jax.ShapeDtypeStruct((req, rows, 1), jnp.float32),
                   jax.ShapeDtypeStruct((req, rows, 1), jnp.float32),
                   jax.ShapeDtypeStruct((req, rows, head_dim), jnp.float32)),
        grid_spec=pltpu.PrefetchScalarGridSpec(
            num_scalar_prefetch=2, grid=grid,
            in_specs=[pl.BlockSpec((BLOCK_REQ, rows, width), blk),
                      pl.BlockSpec((BLOCK_REQ, shard_len, width), blk),
                      pl.BlockSpec((BLOCK_REQ, shard_len, width), blk)],
            out_specs=[pl.BlockSpec((BLOCK_REQ, rows, 1), blk),
                       pl.BlockSpec((BLOCK_REQ, rows, 1), blk),
                       pl.BlockSpec((BLOCK_REQ, rows, head_dim), blk)]),
    )(start, lengths, spread, keys, values)


def attend_shard(query_sel, keys_sel, values_sel, lengths_sel, offsets_sel, slot_base):
    step_count, request_count, local_kv, group_size, head_dim = query_sel.shape
    query_rows = jnp.transpose(query_sel, (1, 2, 0, 3, 4)).reshape(
        request_count, local_kv, step_count * group_size, head_dim
    )
    blank = jnp.zeros((request_count, step_count * group_size, head_dim), query_sel.dtype)
    spread = jnp.concatenate(
        [
            jnp.concatenate([query_rows[:, k] if j == k else blank for j in range(local_kv)], axis=-1)
            for k in range(local_kv)
        ],
        axis=1,
    )
    start = (slot_base - offsets_sel) % S_CAP
    top_part, total_part, mixed_part = cache_attention(
        start, lengths_sel, spread, keys_sel, values_sel, head_dim
    )
    shape = (request_count, local_kv, step_count, group_size)
    return (top_part.reshape(shape), total_part.reshape(shape), mixed_part.reshape(shape + (head_dim,)))


def local(
    hidden_in,
    lengths,
    request_perm,
    k_cache,
    v_cache,
    attn_gain,
    w_query,
    w_key,
    w_value,
    w_out,
    mlp_gain,
    w_gate,
    w_up,
    w_down,
):
    step_count, request_count, model_width = hidden_in.shape
    row_total = step_count * request_count
    group_size = H // KVH
    local_kv = k_cache.shape[2] // HD
    local_heads = local_kv * group_size
    shard_len = k_cache.shape[1]
    flat_in = hidden_in.reshape(row_total, model_width)
    normed = rms_norm(flat_in, attn_gain)
    positions = lengths[None, :] + jnp.arange(step_count, dtype=jnp.int32)[:, None]
    query_raw = jnp.dot(normed, w_query, preferred_element_type=jnp.float32).reshape(
        step_count, request_count, local_heads, HD
    )
    key_raw = jnp.dot(normed, w_key, preferred_element_type=jnp.float32).reshape(
        step_count, request_count, local_kv, HD
    )
    value_new = (
        jnp.dot(normed, w_value, preferred_element_type=jnp.float32)
        .astype(jnp.bfloat16)
        .reshape(step_count, request_count, local_kv, HD)
    )
    queries = (
        rotate(query_raw, positions)
        .astype(jnp.bfloat16)
        .reshape(step_count, request_count, local_kv, group_size, HD)
    )
    key_new = rotate(key_raw, positions).astype(jnp.bfloat16)
    offsets = request_perm * S_CAP // request_count
    slot_base = lax.axis_index("seq") * shard_len
    top_part, total_part, mixed_part = attend_shard(
        queries, k_cache, v_cache, lengths, offsets, slot_base
    )

    levels = (CORE, ZAX, XAX)
    packed = jnp.concatenate([mixed_part, top_part[..., None], total_part[..., None]], axis=-1)
    packed = packed.reshape((2, 4, 4, -1) + packed.shape[1:])
    for level in levels:
        packed = softmax_scatter(level, packed)
    top_s = packed[..., HD]
    total_s = packed[..., HD + 1]
    mixed_s = packed[..., :HD]
    own_count = top_s.shape[0]
    first_req = ((coord(CORE) * 4 + coord(ZAX)) * 4 + coord(XAX)) * own_count

    def own(x):
        return lax.dynamic_slice_in_dim(x, first_req, own_count, axis=1)

    queries_own = own(queries)
    key_own = own(key_new)
    value_own = own(value_new)
    causal = jnp.arange(step_count)[None, :] <= jnp.arange(step_count)[:, None]
    causal_full = causal[None, None, :, None, :]
    new_scores = (
        jnp.einsum("trkgd,urkd->rktgu", queries_own, key_own, preferred_element_type=jnp.float32)
        * attn_scale
    )
    top_new = jnp.max(jnp.where(causal_full, new_scores, neg_large), axis=-1)
    top_final = jnp.maximum(top_s, top_new)
    new_weights = jnp.where(causal_full, jnp.exp(new_scores - top_final[..., None]), 0.0)
    new_mixed = jnp.einsum(
        "rktgu,urkd->rktgd",
        new_weights.astype(jnp.bfloat16),
        value_own,
        preferred_element_type=jnp.float32,
    )
    weight_cache = jnp.exp(top_s - top_final)
    denominator = total_s * weight_cache + jnp.sum(new_weights, axis=-1)
    heads = (mixed_s * weight_cache[..., None] + new_mixed) / denominator[..., None]
    heads = (
        jnp.transpose(heads, (2, 0, 1, 3, 4))
        .reshape(step_count * own_count, local_heads * HD)
        .astype(jnp.bfloat16)
    )
    attended_part = jnp.dot(heads, w_out, preferred_element_type=jnp.float32).reshape(
        step_count, own_count, model_width
    )
    attended = sum_scatter_abs(attended_part, YAX)
    step_own = coord(YAX)
    hidden_own = lax.dynamic_slice_in_dim(take(hidden_in, step_own), first_req, own_count, axis=0)
    residual = (hidden_own.astype(jnp.float32) + branch_scale * attended).astype(jnp.bfloat16)
    normed_mlp = rms_norm(residual, mlp_gain)

    gather_levels = (YAX, XAX, ZAX, CORE)
    rows = normed_mlp
    for level in gather_levels:
        rows = gather_rel(rows, level)
    block_shape = rows.shape[:-1]
    rows = rows.reshape(-1, model_width)
    contract_rows = (((1,), (1,)), ((), ()))
    gate = lax.dot_general(rows, w_gate, contract_rows, preferred_element_type=jnp.float32)
    up_proj = lax.dot_general(rows, w_up, contract_rows, preferred_element_type=jnp.float32)
    hidden = (jax.nn.silu(gate) * up_proj).astype(jnp.bfloat16)
    feed_forward = jnp.dot(hidden, w_down, preferred_element_type=jnp.float32).reshape(
        block_shape + (model_width,)
    )
    for level in reversed(gather_levels):
        feed_forward = sum_scatter_rel(feed_forward, level)
    output = (residual.astype(jnp.float32) + branch_scale * feed_forward).astype(jnp.bfloat16)

    out_rows = output
    for level in gather_levels:
        out_rows = gather_rel(out_rows, level)
    order_levels = (YAX, CORE, ZAX, XAX)
    block_rows = out_rows.shape[4]
    blocks = out_rows.reshape(-1, block_rows * model_width)
    dest = jnp.arange(blocks.shape[0], dtype=jnp.int32)
    member = {}
    for level in reversed(order_levels):
        member[level] = dest % level[2]
        dest = dest // level[2]
    source = jnp.zeros_like(dest)
    for level in (CORE, ZAX, XAX, YAX):
        size = level[2]
        source = source * size + (coord(level) - member[level]) % size
    one_hot = (source[:, None] == jnp.arange(blocks.shape[0], dtype=jnp.int32)[None, :]).astype(
        blocks.dtype
    )
    hidden_out = (
        jnp.dot(one_hot, blocks, preferred_element_type=jnp.float32)
        .astype(jnp.bfloat16)
        .reshape(step_count, request_count, model_width)
    )
    key_out = key_new.reshape(step_count, request_count, local_kv * HD)
    value_out = value_new.reshape(step_count, request_count, local_kv * HD)
    return (hidden_out, key_out, value_out)


def solution(mesh):
    placed = (
        P(),
        P(),
        P(),
        P(None, "seq", "tp"),
        P(None, "seq", "tp"),
        P(),
        P(None, "tp"),
        P(None, "tp"),
        P(None, "tp"),
        P("tp", None),
        P(),
        P(("seq", "tp"), None),
        P(("seq", "tp"), None),
        P(("seq", "tp"), None),
    )
    return jax.shard_map(
        local,
        mesh=mesh,
        in_specs=placed,
        out_specs=(P(), P(None, None, "tp"), P(None, None, "tp")),
        check_vma=False,
    )
```

```python
import math

import jax
import jax.numpy as jnp
from jax import lax
from jax.experimental import pallas as pl
from jax.experimental.pallas import tpu as pltpu
from jax.sharding import PartitionSpec as P

H = 32
KVH = 8
HD = 64
S_CAP = 16384


norm_eps = 1e-05
rope_theta = 10000000.0
attn_scale = 0.015625
branch_scale = 0.5
neg_large = -1e30

CORE = ("seq", 1, 2)
ZAX = ("seq", 2, 4)
XAX = ("seq", 8, 4)
YAX = ("tp", 1, 4)
AXIS_SIZE = {"seq": 32, "tp": 4}


def coord(level):
    axis, stride, size = level
    return (lax.axis_index(axis) // stride) % size


def shift_perm(level, d):
    axis, stride, size = level
    pairs = []
    for i in range(AXIS_SIZE[axis]):
        c = (i // stride) % size
        pairs.append((i, i + ((c + d) % size - c) * stride))
    return pairs


def shifted(x, level, d):
    return lax.ppermute(x, level[0], shift_perm(level, d))


def take(x, index):
    return lax.dynamic_index_in_dim(x, index, axis=0, keepdims=False)


def softmax_scatter(level, packed):
    size = level[2]
    c = coord(level)
    parts = [take(packed, c)]
    for d in range(1, size):
        parts.append(shifted(take(packed, (c + d) % size), level, d))
    head_dim = packed.shape[-1] - 2
    top_all = parts[0][..., head_dim]
    for p in parts[1:]:
        top_all = jnp.maximum(top_all, p[..., head_dim])
    total_all = 0.0
    mixed_all = 0.0
    for p in parts:
        factor = jnp.exp(p[..., head_dim] - top_all)
        total_all = total_all + p[..., head_dim + 1] * factor
        mixed_all = mixed_all + p[..., :head_dim] * factor[..., None]
    return jnp.concatenate([mixed_all, top_all[..., None], total_all[..., None]], axis=-1)


def sum_scatter_abs(x, level):
    size = level[2]
    c = coord(level)
    acc = take(x, c)
    for d in range(1, size):
        acc = acc + shifted(take(x, (c + d) % size), level, d)
    return acc


def sum_all_ordered(x, level):
    size = level[2]
    c = coord(level)
    parts = [x] + [shifted(x, level, d) for d in range(1, size)]
    total = None
    for m in range(size):
        part = parts[0]
        for d in range(1, size):
            part = jnp.where((c - d) % size == m, parts[d], part)
        total = part if total is None else total + part
    return total


def gather_rel(x, level):
    size = level[2]
    parts = [x] + [shifted(x, level, d) for d in range(1, size)]
    return jnp.stack(parts, axis=0)


def sum_scatter_rel(x, level):
    size = level[2]
    acc = x[0]
    for d in range(1, size):
        acc = acc + shifted(x[size - d], level, d)
    return acc


def rms_norm(values, gain_vector):
    floats = values.astype(jnp.float32)
    square_mean = jnp.mean(floats * floats, axis=-1, keepdims=True)
    return (floats * lax.rsqrt(square_mean + norm_eps) * gain_vector.astype(jnp.float32)).astype(
        jnp.bfloat16
    )


def rotate(vectors, positions):
    half_size = vectors.shape[-1] // 2
    inverse = jnp.exp(
        jnp.arange(half_size, dtype=jnp.float32) * (-2.0 * math.log(rope_theta) / vectors.shape[-1])
    )
    angles = positions.astype(jnp.float32)[..., None] * inverse
    cosine = jnp.cos(angles)[..., None, :]
    sine = jnp.sin(angles)[..., None, :]
    first_half = vectors[..., :half_size]
    second_half = vectors[..., half_size:]
    return jnp.concatenate(
        [first_half * cosine - second_half * sine, second_half * cosine + first_half * sine],
        axis=-1,
    )


BLOCK_REQ = 8


def cache_kernel(start_ref, len_ref, q_ref, k_ref, v_ref, top_ref, total_ref, mixed_ref):
    block = pl.program_id(0)
    rows = q_ref.shape[1]
    half = rows // 2
    head_dim = mixed_ref.shape[2]
    shard_len = k_ref.shape[1]
    slots = lax.broadcasted_iota(jnp.int32, (1, shard_len), 1)
    for i in range(q_ref.shape[0]):
        r = block * q_ref.shape[0] + i
        rel = slots + start_ref[r]
        rel = jnp.where(rel >= S_CAP, rel - S_CAP, rel)
        live = rel < len_ref[r]
        scores = lax.dot_general(q_ref[i], k_ref[i], (((1,), (1,)), ((), ())),
                                 preferred_element_type=jnp.float32) * attn_scale
        top = jnp.max(jnp.where(live, scores, neg_large), axis=-1, keepdims=True)
        weights = jnp.where(live, jnp.exp(scores - top), 0.0)
        top_ref[i] = top
        total_ref[i] = jnp.sum(weights, axis=-1, keepdims=True)
        mixed = jnp.dot(weights.astype(jnp.bfloat16), v_ref[i], preferred_element_type=jnp.float32)
        mixed_ref[i, 0:half, :] = mixed[0:half, 0:head_dim]
        mixed_ref[i, half:rows, :] = mixed[half:rows, head_dim:2 * head_dim]


def cache_attention(start, lengths, spread, keys, values, head_dim):
    req, rows, width = spread.shape
    shard_len = keys.shape[1]
    grid = (req // BLOCK_REQ,)
    def blk(b, s, l):
        return (b, 0, 0)
    return pl.pallas_call(
        cache_kernel,
        out_shape=(jax.ShapeDtypeStruct((req, rows, 1), jnp.float32),
                   jax.ShapeDtypeStruct((req, rows, 1), jnp.float32),
                   jax.ShapeDtypeStruct((req, rows, head_dim), jnp.float32)),
        grid_spec=pltpu.PrefetchScalarGridSpec(
            num_scalar_prefetch=2, grid=grid,
            in_specs=[pl.BlockSpec((BLOCK_REQ, rows, width), blk),
                      pl.BlockSpec((BLOCK_REQ, shard_len, width), blk),
                      pl.BlockSpec((BLOCK_REQ, shard_len, width), blk)],
            out_specs=[pl.BlockSpec((BLOCK_REQ, rows, 1), blk),
                       pl.BlockSpec((BLOCK_REQ, rows, 1), blk),
                       pl.BlockSpec((BLOCK_REQ, rows, head_dim), blk)]),
    )(start, lengths, spread, keys, values)


def attend_shard(query_sel, keys_sel, values_sel, lengths_sel, offsets_sel, slot_base):
    step_count, request_count, local_kv, group_size, head_dim = query_sel.shape
    query_rows = jnp.transpose(query_sel, (1, 2, 0, 3, 4)).reshape(
        request_count, local_kv, step_count * group_size, head_dim
    )
    blank = jnp.zeros((request_count, step_count * group_size, head_dim), query_sel.dtype)
    spread = jnp.concatenate(
        [
            jnp.concatenate([query_rows[:, k] if j == k else blank for j in range(local_kv)], axis=-1)
            for k in range(local_kv)
        ],
        axis=1,
    )
    start = (slot_base - offsets_sel) % S_CAP
    top_part, total_part, mixed_part = cache_attention(
        start, lengths_sel, spread, keys_sel, values_sel, head_dim
    )
    shape = (request_count, local_kv, step_count, group_size)
    return (top_part.reshape(shape), total_part.reshape(shape), mixed_part.reshape(shape + (head_dim,)))


def local(
    hidden_in,
    lengths,
    request_perm,
    k_cache,
    v_cache,
    attn_gain,
    w_query,
    w_key,
    w_value,
    w_out,
    mlp_gain,
    w_gate,
    w_up,
    w_down,
):
    step_count, request_count, model_width = hidden_in.shape
    row_total = step_count * request_count
    group_size = H // KVH
    local_kv = k_cache.shape[2] // HD
    local_heads = local_kv * group_size
    shard_len = k_cache.shape[1]
    flat_in = hidden_in.reshape(row_total, model_width)
    normed = rms_norm(flat_in, attn_gain)
    positions = lengths[None, :] + jnp.arange(step_count, dtype=jnp.int32)[:, None]
    query_raw = jnp.dot(normed, w_query, preferred_element_type=jnp.float32).reshape(
        step_count, request_count, local_heads, HD
    )
    key_raw = jnp.dot(normed, w_key, preferred_element_type=jnp.float32).reshape(
        step_count, request_count, local_kv, HD
    )
    value_new = (
        jnp.dot(normed, w_value, preferred_element_type=jnp.float32)
        .astype(jnp.bfloat16)
        .reshape(step_count, request_count, local_kv, HD)
    )
    queries = (
        rotate(query_raw, positions)
        .astype(jnp.bfloat16)
        .reshape(step_count, request_count, local_kv, group_size, HD)
    )
    key_new = rotate(key_raw, positions).astype(jnp.bfloat16)
    offsets = request_perm * S_CAP // request_count
    slot_base = lax.axis_index("seq") * shard_len
    top_part, total_part, mixed_part = attend_shard(
        queries, k_cache, v_cache, lengths, offsets, slot_base
    )

    levels = (CORE, ZAX, XAX)
    packed = jnp.concatenate([mixed_part, top_part[..., None], total_part[..., None]], axis=-1)
    packed = packed.reshape((2, 4, 4, -1) + packed.shape[1:])
    for level in levels:
        packed = softmax_scatter(level, packed)
    top_s = packed[..., HD]
    total_s = packed[..., HD + 1]
    mixed_s = packed[..., :HD]
    own_count = top_s.shape[0]
    first_req = ((coord(CORE) * 4 + coord(ZAX)) * 4 + coord(XAX)) * own_count

    def own(x):
        return lax.dynamic_slice_in_dim(x, first_req, own_count, axis=1)

    queries_own = own(queries)
    key_own = own(key_new)
    value_own = own(value_new)
    causal = jnp.arange(step_count)[None, :] <= jnp.arange(step_count)[:, None]
    causal_full = causal[None, None, :, None, :]
    new_scores = (
        jnp.einsum("trkgd,urkd->rktgu", queries_own, key_own, preferred_element_type=jnp.float32)
        * attn_scale
    )
    top_new = jnp.max(jnp.where(causal_full, new_scores, neg_large), axis=-1)
    top_final = jnp.maximum(top_s, top_new)
    new_weights = jnp.where(causal_full, jnp.exp(new_scores - top_final[..., None]), 0.0)
    new_mixed = jnp.einsum(
        "rktgu,urkd->rktgd",
        new_weights.astype(jnp.bfloat16),
        value_own,
        preferred_element_type=jnp.float32,
    )
    weight_cache = jnp.exp(top_s - top_final)
    denominator = total_s * weight_cache + jnp.sum(new_weights, axis=-1)
    heads = (mixed_s * weight_cache[..., None] + new_mixed) / denominator[..., None]
    heads = (
        jnp.transpose(heads, (2, 0, 1, 3, 4))
        .reshape(step_count * own_count, local_heads * HD)
        .astype(jnp.bfloat16)
    )
    attended_part = jnp.dot(heads, w_out, preferred_element_type=jnp.float32).reshape(
        step_count, own_count, model_width
    )
    attended = sum_all_ordered(attended_part, YAX)
    hidden_own = lax.dynamic_slice_in_dim(hidden_in, first_req, own_count, axis=1)
    residual = (hidden_own.astype(jnp.float32) + branch_scale * attended).astype(jnp.bfloat16)
    normed_mlp = rms_norm(residual, mlp_gain)

    gather_levels = (XAX, ZAX, CORE)
    rows = normed_mlp
    for level in gather_levels:
        rows = gather_rel(rows, level)
    block_shape = rows.shape[:-1]
    rows = rows.reshape(-1, model_width)
    contract_rows = (((1,), (1,)), ((), ()))
    gate = lax.dot_general(rows, w_gate, contract_rows, preferred_element_type=jnp.float32)
    up_proj = lax.dot_general(rows, w_up, contract_rows, preferred_element_type=jnp.float32)
    hidden = (jax.nn.silu(gate) * up_proj).astype(jnp.bfloat16)
    feed_forward = jnp.dot(hidden, w_down, preferred_element_type=jnp.float32).reshape(
        block_shape + (model_width,)
    )
    for level in reversed(gather_levels):
        feed_forward = sum_scatter_rel(feed_forward, level)
    feed_forward = sum_all_ordered(feed_forward, YAX)
    output = (residual.astype(jnp.float32) + branch_scale * feed_forward).astype(jnp.bfloat16)

    out_rows = output
    for level in gather_levels:
        out_rows = gather_rel(out_rows, level)
    block_rows = out_rows.shape[4]
    blocks = out_rows.reshape(-1, block_rows * model_width)
    dest = jnp.arange(blocks.shape[0], dtype=jnp.int32)
    member = {}
    for level in (XAX, ZAX, CORE):
        member[level] = dest % level[2]
        dest = dest // level[2]
    step_of = dest % step_count
    source = jnp.zeros_like(dest)
    for level in (CORE, ZAX, XAX):
        size = level[2]
        source = source * size + (coord(level) - member[level]) % size
    source = source * step_count + step_of
    one_hot = (source[:, None] == jnp.arange(blocks.shape[0], dtype=jnp.int32)[None, :]).astype(
        blocks.dtype
    )
    hidden_out = (
        jnp.dot(one_hot, blocks, preferred_element_type=jnp.float32)
        .astype(jnp.bfloat16)
        .reshape(step_count, request_count, model_width)
    )
    key_out = key_new.reshape(step_count, request_count, local_kv * HD)
    value_out = value_new.reshape(step_count, request_count, local_kv * HD)
    return (hidden_out, key_out, value_out)


def solution(mesh):
    placed = (
        P(),
        P(),
        P(),
        P(None, "seq", "tp"),
        P(None, "seq", "tp"),
        P(),
        P(None, "tp"),
        P(None, "tp"),
        P(None, "tp"),
        P("tp", None),
        P(),
        P(("seq", "tp"), None),
        P(("seq", "tp"), None),
        P(("seq", "tp"), None),
    )
    return jax.shard_map(
        local,
        mesh=mesh,
        in_specs=placed,
        out_specs=(P(), P(None, None, "tp"), P(None, None, "tp")),
        check_vma=False,
    )
```

```python
import math

import jax
import jax.numpy as jnp
from jax import lax
from jax.experimental import pallas as pl
from jax.experimental.pallas import tpu as pltpu
from jax.sharding import PartitionSpec as P

H = 32
KVH = 8
HD = 64
S_CAP = 16384


norm_eps = 1e-05
rope_theta = 10000000.0
attn_scale = 0.015625
branch_scale = 0.5
neg_large = -1e30

CORE = ("seq", 1, 2)
ZAX = ("seq", 2, 4)
XAX = ("seq", 8, 4)
YAX = ("tp", 1, 4)
AXIS_SIZE = {"seq": 32, "tp": 4}


def coord(level):
    axis, stride, size = level
    return (lax.axis_index(axis) // stride) % size


def shift_perm(level, d):
    axis, stride, size = level
    pairs = []
    for i in range(AXIS_SIZE[axis]):
        c = (i // stride) % size
        pairs.append((i, i + ((c + d) % size - c) * stride))
    return pairs


def shifted(x, level, d):
    return lax.ppermute(x, level[0], shift_perm(level, d))


def take(x, index):
    return lax.dynamic_index_in_dim(x, index, axis=0, keepdims=False)


def softmax_scatter(level, packed):
    size = level[2]
    c = coord(level)
    parts = [take(packed, c)]
    for d in range(1, size):
        parts.append(shifted(take(packed, (c + d) % size), level, d))
    head_dim = packed.shape[-1] - 2
    top_all = parts[0][..., head_dim]
    for p in parts[1:]:
        top_all = jnp.maximum(top_all, p[..., head_dim])
    total_all = 0.0
    mixed_all = 0.0
    for p in parts:
        factor = jnp.exp(p[..., head_dim] - top_all)
        total_all = total_all + p[..., head_dim + 1] * factor
        mixed_all = mixed_all + p[..., :head_dim] * factor[..., None]
    return jnp.concatenate([mixed_all, top_all[..., None], total_all[..., None]], axis=-1)


def sum_scatter_abs(x, level):
    size = level[2]
    c = coord(level)
    acc = take(x, c)
    for d in range(1, size):
        acc = acc + shifted(take(x, (c + d) % size), level, d)
    return acc


def sum_all_ordered(x, level):
    size = level[2]
    c = coord(level)
    parts = [x] + [shifted(x, level, d) for d in range(1, size)]
    total = None
    for m in range(size):
        part = parts[0]
        for d in range(1, size):
            part = jnp.where((c - d) % size == m, parts[d], part)
        total = part if total is None else total + part
    return total


def gather_rel(x, level):
    size = level[2]
    parts = [x] + [shifted(x, level, d) for d in range(1, size)]
    return jnp.stack(parts, axis=0)


def sum_scatter_rel(x, level):
    size = level[2]
    acc = x[0]
    for d in range(1, size):
        acc = acc + shifted(x[size - d], level, d)
    return acc


def rms_norm(values, gain_vector):
    floats = values.astype(jnp.float32)
    square_mean = jnp.mean(floats * floats, axis=-1, keepdims=True)
    return (floats * lax.rsqrt(square_mean + norm_eps) * gain_vector.astype(jnp.float32)).astype(
        jnp.bfloat16
    )


def rotate(vectors, positions):
    half_size = vectors.shape[-1] // 2
    inverse = jnp.exp(
        jnp.arange(half_size, dtype=jnp.float32) * (-2.0 * math.log(rope_theta) / vectors.shape[-1])
    )
    angles = positions.astype(jnp.float32)[..., None] * inverse
    cosine = jnp.cos(angles)[..., None, :]
    sine = jnp.sin(angles)[..., None, :]
    first_half = vectors[..., :half_size]
    second_half = vectors[..., half_size:]
    return jnp.concatenate(
        [first_half * cosine - second_half * sine, second_half * cosine + first_half * sine],
        axis=-1,
    )


BLOCK_REQ = 8


def cache_kernel(start_ref, len_ref, q_ref, k_ref, v_ref, packed_ref):
    block = pl.program_id(0)
    rows = q_ref.shape[1]
    half = rows // 2
    head_dim = packed_ref.shape[2] - 2
    shard_len = k_ref.shape[1]
    slots = lax.broadcasted_iota(jnp.int32, (1, shard_len), 1)
    for i in range(q_ref.shape[0]):
        r = block * q_ref.shape[0] + i
        rel = slots + start_ref[r]
        rel = jnp.where(rel >= S_CAP, rel - S_CAP, rel)
        live = rel < len_ref[r]
        scores = lax.dot_general(q_ref[i], k_ref[i], (((1,), (1,)), ((), ())),
                                 preferred_element_type=jnp.float32) * attn_scale
        top = jnp.max(jnp.where(live, scores, neg_large), axis=-1, keepdims=True)
        weights = jnp.where(live, jnp.exp(scores - top), 0.0)
        packed_ref[i, :, head_dim:head_dim + 1] = top
        packed_ref[i, :, head_dim + 1:head_dim + 2] = jnp.sum(weights, axis=-1, keepdims=True)
        mixed = jnp.dot(weights.astype(jnp.bfloat16), v_ref[i], preferred_element_type=jnp.float32)
        packed_ref[i, 0:half, 0:head_dim] = mixed[0:half, 0:head_dim]
        packed_ref[i, half:rows, 0:head_dim] = mixed[half:rows, head_dim:2 * head_dim]


def cache_attention(start, lengths, spread, keys, values, head_dim):
    req, rows, width = spread.shape
    shard_len = keys.shape[1]
    grid = (req // BLOCK_REQ,)
    def blk(b, s, l):
        return (b, 0, 0)
    return pl.pallas_call(
        cache_kernel,
        out_shape=jax.ShapeDtypeStruct((req, rows, head_dim + 2), jnp.float32),
        grid_spec=pltpu.PrefetchScalarGridSpec(
            num_scalar_prefetch=2, grid=grid,
            in_specs=[pl.BlockSpec((BLOCK_REQ, rows, width), blk),
                      pl.BlockSpec((BLOCK_REQ, shard_len, width), blk),
                      pl.BlockSpec((BLOCK_REQ, shard_len, width), blk)],
            out_specs=pl.BlockSpec((BLOCK_REQ, rows, head_dim + 2), blk)),
    )(start, lengths, spread, keys, values)


def attend_shard(query_sel, keys_sel, values_sel, lengths_sel, offsets_sel, slot_base):
    step_count, request_count, local_kv, group_size, head_dim = query_sel.shape
    query_rows = jnp.transpose(query_sel, (1, 2, 0, 3, 4)).reshape(
        request_count, local_kv, step_count * group_size, head_dim
    )
    blank = jnp.zeros((request_count, step_count * group_size, head_dim), query_sel.dtype)
    spread = jnp.concatenate(
        [
            jnp.concatenate([query_rows[:, k] if j == k else blank for j in range(local_kv)], axis=-1)
            for k in range(local_kv)
        ],
        axis=1,
    )
    start = (slot_base - offsets_sel) % S_CAP
    return cache_attention(start, lengths_sel, spread, keys_sel, values_sel, head_dim)


def local(
    hidden_in,
    lengths,
    request_perm,
    k_cache,
    v_cache,
    attn_gain,
    w_query,
    w_key,
    w_value,
    w_out,
    mlp_gain,
    w_gate,
    w_up,
    w_down,
):
    step_count, request_count, model_width = hidden_in.shape
    row_total = step_count * request_count
    group_size = H // KVH
    local_kv = k_cache.shape[2] // HD
    local_heads = local_kv * group_size
    shard_len = k_cache.shape[1]
    flat_in = hidden_in.reshape(row_total, model_width)
    normed = rms_norm(flat_in, attn_gain)
    positions = lengths[None, :] + jnp.arange(step_count, dtype=jnp.int32)[:, None]
    query_raw = jnp.dot(normed, w_query, preferred_element_type=jnp.float32).reshape(
        step_count, request_count, local_heads, HD
    )
    key_raw = jnp.dot(normed, w_key, preferred_element_type=jnp.float32).reshape(
        step_count, request_count, local_kv, HD
    )
    value_new = (
        jnp.dot(normed, w_value, preferred_element_type=jnp.float32)
        .astype(jnp.bfloat16)
        .reshape(step_count, request_count, local_kv, HD)
    )
    queries = (
        rotate(query_raw, positions)
        .astype(jnp.bfloat16)
        .reshape(step_count, request_count, local_kv, group_size, HD)
    )
    key_new = rotate(key_raw, positions).astype(jnp.bfloat16)
    offsets = request_perm * S_CAP // request_count
    slot_base = lax.axis_index("seq") * shard_len
    packed = attend_shard(queries, k_cache, v_cache, lengths, offsets, slot_base)

    levels = (CORE, ZAX, XAX)
    packed = packed.reshape((2, 4, 4, -1) + packed.shape[1:])
    for level in levels:
        packed = softmax_scatter(level, packed)
    own_shape = (packed.shape[0], local_kv, step_count, group_size)
    top_s = packed[..., HD].reshape(own_shape)
    total_s = packed[..., HD + 1].reshape(own_shape)
    mixed_s = packed[..., :HD].reshape(own_shape + (HD,))
    own_count = top_s.shape[0]
    first_req = ((coord(CORE) * 4 + coord(ZAX)) * 4 + coord(XAX)) * own_count

    def own(x):
        return lax.dynamic_slice_in_dim(x, first_req, own_count, axis=1)

    queries_own = own(queries)
    key_own = own(key_new)
    value_own = own(value_new)
    causal = jnp.arange(step_count)[None, :] <= jnp.arange(step_count)[:, None]
    causal_full = causal[None, None, :, None, :]
    new_scores = (
        jnp.einsum("trkgd,urkd->rktgu", queries_own, key_own, preferred_element_type=jnp.float32)
        * attn_scale
    )
    top_new = jnp.max(jnp.where(causal_full, new_scores, neg_large), axis=-1)
    top_final = jnp.maximum(top_s, top_new)
    new_weights = jnp.where(causal_full, jnp.exp(new_scores - top_final[..., None]), 0.0)
    new_mixed = jnp.einsum(
        "rktgu,urkd->rktgd",
        new_weights.astype(jnp.bfloat16),
        value_own,
        preferred_element_type=jnp.float32,
    )
    weight_cache = jnp.exp(top_s - top_final)
    denominator = total_s * weight_cache + jnp.sum(new_weights, axis=-1)
    heads = (mixed_s * weight_cache[..., None] + new_mixed) / denominator[..., None]
    heads = (
        jnp.transpose(heads, (2, 0, 1, 3, 4))
        .reshape(step_count * own_count, local_heads * HD)
        .astype(jnp.bfloat16)
    )
    attended_part = jnp.dot(heads, w_out, preferred_element_type=jnp.float32).reshape(
        step_count, own_count, model_width
    )
    attended = sum_all_ordered(attended_part, YAX)
    hidden_own = lax.dynamic_slice_in_dim(hidden_in, first_req, own_count, axis=1)
    residual = (hidden_own.astype(jnp.float32) + branch_scale * attended).astype(jnp.bfloat16)
    normed_mlp = rms_norm(residual, mlp_gain)

    gather_levels = (XAX, ZAX)
    rows = normed_mlp
    for level in gather_levels:
        rows = gather_rel(rows, level)
    halves = (rows, shifted(rows, CORE, 1))
    block_shape = rows.shape[:-1]
    contract_rows = (((1,), (1,)), ((), ()))

    def feed(half_rows):
        flat = half_rows.reshape(-1, model_width)
        gate = lax.dot_general(flat, w_gate, contract_rows, preferred_element_type=jnp.float32)
        up_proj = lax.dot_general(flat, w_up, contract_rows, preferred_element_type=jnp.float32)
        hidden = (jax.nn.silu(gate) * up_proj).astype(jnp.bfloat16)
        return jnp.dot(hidden, w_down, preferred_element_type=jnp.float32).reshape(
            block_shape + (model_width,)
        )

    feed_forward = feed(halves[0]) + shifted(feed(halves[1]), CORE, 1)
    for level in reversed(gather_levels):
        feed_forward = sum_scatter_rel(feed_forward, level)
    feed_forward = sum_all_ordered(feed_forward, YAX)
    output = (residual.astype(jnp.float32) + branch_scale * feed_forward).astype(jnp.bfloat16)

    out_rows = output
    for level in gather_levels:
        out_rows = gather_rel(out_rows, level)
    out_halves = (out_rows, shifted(out_rows, CORE, 1))
    block_rows = out_rows.shape[3]
    half_blocks = [h.reshape(-1, block_rows * model_width) for h in out_halves]
    half_count = half_blocks[0].shape[0]
    dest = jnp.arange(2 * half_count, dtype=jnp.int32)
    member = {}
    for level in (XAX, ZAX, CORE):
        member[level] = dest % level[2]
        dest = dest // level[2]
    step_of = dest % step_count
    source = jnp.zeros_like(dest)
    for level in (CORE, ZAX, XAX):
        size = level[2]
        source = source * size + (coord(level) - member[level]) % size
    source = source * step_count + step_of
    merged = 0.0
    for kc, blocks in enumerate(half_blocks):
        cols = kc * half_count + jnp.arange(half_count, dtype=jnp.int32)
        one_hot = (source[:, None] == cols[None, :]).astype(blocks.dtype)
        merged = merged + jnp.dot(one_hot, blocks, preferred_element_type=jnp.float32)
    hidden_out = merged.astype(jnp.bfloat16).reshape(step_count, request_count, model_width)
    key_out = key_new.reshape(step_count, request_count, local_kv * HD)
    value_out = value_new.reshape(step_count, request_count, local_kv * HD)
    return (hidden_out, key_out, value_out)


def solution(mesh):
    placed = (
        P(),
        P(),
        P(),
        P(None, "seq", "tp"),
        P(None, "seq", "tp"),
        P(),
        P(None, "tp"),
        P(None, "tp"),
        P(None, "tp"),
        P("tp", None),
        P(),
        P(("seq", "tp"), None),
        P(("seq", "tp"), None),
        P(("seq", "tp"), None),
    )
    return jax.shard_map(
        local,
        mesh=mesh,
        in_specs=placed,
        out_specs=(P(), P(None, None, "tp"), P(None, None, "tp")),
        check_vma=False,
    )
```

```python
import math

import jax
import jax.numpy as jnp
from jax import lax
from jax.experimental import pallas as pl
from jax.experimental.pallas import tpu as pltpu
from jax.sharding import PartitionSpec as P

H = 32
KVH = 8
HD = 64
S_CAP = 16384


norm_eps = 1e-05
rope_theta = 10000000.0
attn_scale = 0.015625
branch_scale = 0.5
neg_large = -1e30

CORE = ("seq", 1, 2)
ZAX = ("seq", 2, 4)
XAX = ("seq", 8, 4)
YAX = ("tp", 1, 4)
AXIS_SIZE = {"seq": 32, "tp": 4}


def coord(level):
    axis, stride, size = level
    return (lax.axis_index(axis) // stride) % size


def shift_perm(level, d):
    axis, stride, size = level
    pairs = []
    for i in range(AXIS_SIZE[axis]):
        c = (i // stride) % size
        pairs.append((i, i + ((c + d) % size - c) * stride))
    return pairs


def shifted(x, level, d):
    return lax.ppermute(x, level[0], shift_perm(level, d))


def take(x, index):
    return lax.dynamic_index_in_dim(x, index, axis=0, keepdims=False)


def softmax_scatter(level, packed):
    size = level[2]
    c = coord(level)
    parts = [take(packed, c)]
    for d in range(1, size):
        parts.append(shifted(take(packed, (c + d) % size), level, d))
    head_dim = packed.shape[-1] - 2
    top_all = parts[0][..., head_dim]
    for p in parts[1:]:
        top_all = jnp.maximum(top_all, p[..., head_dim])
    total_all = 0.0
    mixed_all = 0.0
    for p in parts:
        factor = jnp.exp(p[..., head_dim] - top_all)
        total_all = total_all + p[..., head_dim + 1] * factor
        mixed_all = mixed_all + p[..., :head_dim] * factor[..., None]
    return jnp.concatenate([mixed_all, top_all[..., None], total_all[..., None]], axis=-1)


def sum_scatter_abs(x, level):
    size = level[2]
    c = coord(level)
    acc = take(x, c)
    for d in range(1, size):
        acc = acc + shifted(take(x, (c + d) % size), level, d)
    return acc


def sum_all_ordered(x, level):
    size = level[2]
    c = coord(level)
    parts = [x] + [shifted(x, level, d) for d in range(1, size)]
    total = None
    for m in range(size):
        part = parts[0]
        for d in range(1, size):
            part = jnp.where((c - d) % size == m, parts[d], part)
        total = part if total is None else total + part
    return total


def gather_rel(x, level):
    size = level[2]
    parts = [x] + [shifted(x, level, d) for d in range(1, size)]
    return jnp.stack(parts, axis=0)


def sum_scatter_rel(x, level, wire):
    size = level[2]
    acc = x[0]
    for d in range(1, size):
        acc = acc + shifted(x[size - d].astype(wire), level, d).astype(acc.dtype)
    return acc


def rms_norm(values, gain_vector):
    floats = values.astype(jnp.float32)
    square_mean = jnp.mean(floats * floats, axis=-1, keepdims=True)
    return (floats * lax.rsqrt(square_mean + norm_eps) * gain_vector.astype(jnp.float32)).astype(
        jnp.bfloat16
    )


def rotate(vectors, positions):
    half_size = vectors.shape[-1] // 2
    inverse = jnp.exp(
        jnp.arange(half_size, dtype=jnp.float32) * (-2.0 * math.log(rope_theta) / vectors.shape[-1])
    )
    angles = positions.astype(jnp.float32)[..., None] * inverse
    cosine = jnp.cos(angles)[..., None, :]
    sine = jnp.sin(angles)[..., None, :]
    first_half = vectors[..., :half_size]
    second_half = vectors[..., half_size:]
    return jnp.concatenate(
        [first_half * cosine - second_half * sine, second_half * cosine + first_half * sine],
        axis=-1,
    )


BLOCK_REQ = 8


def cache_kernel(start_ref, len_ref, q_ref, k_ref, v_ref, packed_ref):
    block = pl.program_id(0)
    rows = q_ref.shape[1]
    half = rows // 2
    head_dim = packed_ref.shape[2] - 2
    shard_len = k_ref.shape[1]
    slots = lax.broadcasted_iota(jnp.int32, (1, shard_len), 1)
    for i in range(q_ref.shape[0]):
        r = block * q_ref.shape[0] + i
        rel = slots + start_ref[r]
        rel = jnp.where(rel >= S_CAP, rel - S_CAP, rel)
        live = rel < len_ref[r]
        scores = lax.dot_general(q_ref[i], k_ref[i], (((1,), (1,)), ((), ())),
                                 preferred_element_type=jnp.float32) * attn_scale
        top = jnp.max(jnp.where(live, scores, neg_large), axis=-1, keepdims=True)
        weights = jnp.where(live, jnp.exp(scores - top), 0.0)
        packed_ref[i, :, head_dim:head_dim + 1] = top
        packed_ref[i, :, head_dim + 1:head_dim + 2] = jnp.sum(weights, axis=-1, keepdims=True)
        mixed = jnp.dot(weights.astype(jnp.bfloat16), v_ref[i], preferred_element_type=jnp.float32)
        packed_ref[i, 0:half, 0:head_dim] = mixed[0:half, 0:head_dim]
        packed_ref[i, half:rows, 0:head_dim] = mixed[half:rows, head_dim:2 * head_dim]


def cache_attention(start, lengths, spread, keys, values, head_dim):
    req, rows, width = spread.shape
    shard_len = keys.shape[1]
    grid = (req // BLOCK_REQ,)
    def blk(b, s, l):
        return (b, 0, 0)
    return pl.pallas_call(
        cache_kernel,
        out_shape=jax.ShapeDtypeStruct((req, rows, head_dim + 2), jnp.float32),
        grid_spec=pltpu.PrefetchScalarGridSpec(
            num_scalar_prefetch=2, grid=grid,
            in_specs=[pl.BlockSpec((BLOCK_REQ, rows, width), blk),
                      pl.BlockSpec((BLOCK_REQ, shard_len, width), blk),
                      pl.BlockSpec((BLOCK_REQ, shard_len, width), blk)],
            out_specs=pl.BlockSpec((BLOCK_REQ, rows, head_dim + 2), blk)),
    )(start, lengths, spread, keys, values)


def attend_shard(query_sel, keys_sel, values_sel, lengths_sel, offsets_sel, slot_base):
    step_count, request_count, local_kv, group_size, head_dim = query_sel.shape
    query_rows = jnp.transpose(query_sel, (1, 2, 0, 3, 4)).reshape(
        request_count, local_kv, step_count * group_size, head_dim
    )
    blank = jnp.zeros((request_count, step_count * group_size, head_dim), query_sel.dtype)
    spread = jnp.concatenate(
        [
            jnp.concatenate([query_rows[:, k] if j == k else blank for j in range(local_kv)], axis=-1)
            for k in range(local_kv)
        ],
        axis=1,
    )
    start = (slot_base - offsets_sel) % S_CAP
    return cache_attention(start, lengths_sel, spread, keys_sel, values_sel, head_dim)


def local(
    hidden_in,
    lengths,
    request_perm,
    k_cache,
    v_cache,
    attn_gain,
    w_query,
    w_key,
    w_value,
    w_out,
    mlp_gain,
    w_gate,
    w_up,
    w_down,
):
    step_count, request_count, model_width = hidden_in.shape
    row_total = step_count * request_count
    group_size = H // KVH
    local_kv = k_cache.shape[2] // HD
    local_heads = local_kv * group_size
    shard_len = k_cache.shape[1]
    flat_in = hidden_in.reshape(row_total, model_width)
    normed = rms_norm(flat_in, attn_gain)
    positions = lengths[None, :] + jnp.arange(step_count, dtype=jnp.int32)[:, None]
    query_raw = jnp.dot(normed, w_query, preferred_element_type=jnp.float32).reshape(
        step_count, request_count, local_heads, HD
    )
    key_raw = jnp.dot(normed, w_key, preferred_element_type=jnp.float32).reshape(
        step_count, request_count, local_kv, HD
    )
    value_new = (
        jnp.dot(normed, w_value, preferred_element_type=jnp.float32)
        .astype(jnp.bfloat16)
        .reshape(step_count, request_count, local_kv, HD)
    )
    queries = (
        rotate(query_raw, positions)
        .astype(jnp.bfloat16)
        .reshape(step_count, request_count, local_kv, group_size, HD)
    )
    key_new = rotate(key_raw, positions).astype(jnp.bfloat16)
    offsets = request_perm * S_CAP // request_count
    slot_base = lax.axis_index("seq") * shard_len
    packed = attend_shard(queries, k_cache, v_cache, lengths, offsets, slot_base)

    levels = (CORE, ZAX, XAX)
    packed = packed.reshape((2, 4, 4, -1) + packed.shape[1:])
    for level in levels:
        packed = softmax_scatter(level, packed)
    own_shape = (packed.shape[0], local_kv, step_count, group_size)
    top_s = packed[..., HD].reshape(own_shape)
    total_s = packed[..., HD + 1].reshape(own_shape)
    mixed_s = packed[..., :HD].reshape(own_shape + (HD,))
    own_count = top_s.shape[0]
    first_req = ((coord(CORE) * 4 + coord(ZAX)) * 4 + coord(XAX)) * own_count

    def own(x):
        return lax.dynamic_slice_in_dim(x, first_req, own_count, axis=1)

    queries_own = own(queries)
    key_own = own(key_new)
    value_own = own(value_new)
    causal = jnp.arange(step_count)[None, :] <= jnp.arange(step_count)[:, None]
    causal_full = causal[None, None, :, None, :]
    new_scores = (
        jnp.einsum("trkgd,urkd->rktgu", queries_own, key_own, preferred_element_type=jnp.float32)
        * attn_scale
    )
    top_new = jnp.max(jnp.where(causal_full, new_scores, neg_large), axis=-1)
    top_final = jnp.maximum(top_s, top_new)
    new_weights = jnp.where(causal_full, jnp.exp(new_scores - top_final[..., None]), 0.0)
    new_mixed = jnp.einsum(
        "rktgu,urkd->rktgd",
        new_weights.astype(jnp.bfloat16),
        value_own,
        preferred_element_type=jnp.float32,
    )
    weight_cache = jnp.exp(top_s - top_final)
    denominator = total_s * weight_cache + jnp.sum(new_weights, axis=-1)
    heads = (mixed_s * weight_cache[..., None] + new_mixed) / denominator[..., None]
    heads = (
        jnp.transpose(heads, (2, 0, 1, 3, 4))
        .reshape(step_count * own_count, local_heads * HD)
        .astype(jnp.bfloat16)
    )
    attended_part = jnp.dot(heads, w_out, preferred_element_type=jnp.float32).reshape(
        step_count, own_count, model_width
    )
    attended = sum_all_ordered(attended_part.reshape(-1, model_width), YAX)
    hidden_own = lax.dynamic_slice_in_dim(hidden_in, first_req, own_count, axis=1).reshape(
        -1, model_width
    )
    residual = (hidden_own.astype(jnp.float32) + branch_scale * attended).astype(jnp.bfloat16)
    normed_mlp = rms_norm(residual, mlp_gain)

    gather_levels = (XAX, ZAX)
    rows = normed_mlp
    for level in gather_levels:
        rows = gather_rel(rows, level)
    halves = (rows, shifted(rows, CORE, 1))
    block_shape = rows.shape[:-1]
    contract_rows = (((1,), (1,)), ((), ()))

    def feed(half_rows):
        flat = half_rows.reshape(-1, model_width)
        gate = lax.dot_general(flat, w_gate, contract_rows, preferred_element_type=jnp.float32)
        up_proj = lax.dot_general(flat, w_up, contract_rows, preferred_element_type=jnp.float32)
        hidden = (jax.nn.silu(gate) * up_proj).astype(jnp.bfloat16)
        return jnp.dot(hidden, w_down, preferred_element_type=jnp.float32).reshape(
            block_shape + (model_width,)
        )

    feed_forward = feed(halves[0]) + shifted(feed(halves[1]), CORE, 1)
    for level in reversed(gather_levels):
        feed_forward = sum_scatter_rel(feed_forward, level, jnp.bfloat16)
    feed_forward = sum_all_ordered(feed_forward, YAX)
    output = (residual.astype(jnp.float32) + branch_scale * feed_forward).astype(jnp.bfloat16)

    out_rows = output
    for level in gather_levels:
        out_rows = gather_rel(out_rows, level)
    out_halves = (out_rows, shifted(out_rows, CORE, 1))
    own_rows = out_rows.shape[2]
    half_flat = [h.reshape(-1, model_width) for h in out_halves]
    half_count = half_flat[0].shape[0]
    dest = jnp.arange(2 * half_count, dtype=jnp.int32)
    pair = dest % own_count
    dest = dest // own_count
    member = {}
    for level in (XAX, ZAX, CORE):
        member[level] = dest % level[2]
        dest = dest // level[2]
    step_of = dest % step_count
    source = jnp.zeros_like(dest)
    for level in (CORE, ZAX, XAX):
        size = level[2]
        source = source * size + (coord(level) - member[level]) % size
    source = source * own_rows + step_of * own_count + pair
    merged = 0.0
    for kc, flat in enumerate(half_flat):
        cols = kc * half_count + jnp.arange(half_count, dtype=jnp.int32)
        one_hot = (source[:, None] == cols[None, :]).astype(flat.dtype)
        merged = merged + jnp.dot(one_hot, flat, preferred_element_type=jnp.float32)
    hidden_out = merged.astype(jnp.bfloat16).reshape(step_count, request_count, model_width)
    key_out = key_new.reshape(step_count, request_count, local_kv * HD)
    value_out = value_new.reshape(step_count, request_count, local_kv * HD)
    return (hidden_out, key_out, value_out)


def solution(mesh):
    placed = (
        P(),
        P(),
        P(),
        P(None, "seq", "tp"),
        P(None, "seq", "tp"),
        P(),
        P(None, "tp"),
        P(None, "tp"),
        P(None, "tp"),
        P("tp", None),
        P(),
        P(("seq", "tp"), None),
        P(("seq", "tp"), None),
        P(("seq", "tp"), None),
    )
    return jax.shard_map(
        local,
        mesh=mesh,
        in_specs=placed,
        out_specs=(P(), P(None, None, "tp"), P(None, None, "tp")),
        check_vma=False,
    )
```

```python
import math

import jax
import jax.numpy as jnp
from jax import lax
from jax.experimental import pallas as pl
from jax.experimental.pallas import tpu as pltpu
from jax.sharding import PartitionSpec as P

H = 32
KVH = 8
HD = 64
S_CAP = 16384


norm_eps = 1e-05
rope_theta = 10000000.0
attn_scale = 0.015625
branch_scale = 0.5
neg_large = -1e30

CORE = ("seq", 1, 2)
ZAX = ("seq", 2, 4)
XAX = ("seq", 8, 4)
YAX = ("tp", 1, 4)
AXIS_SIZE = {"seq": 32, "tp": 4}


def coord(level):
    axis, stride, size = level
    return (lax.axis_index(axis) // stride) % size


def shift_perm(level, d):
    axis, stride, size = level
    pairs = []
    for i in range(AXIS_SIZE[axis]):
        c = (i // stride) % size
        pairs.append((i, i + ((c + d) % size - c) * stride))
    return pairs


def shifted(x, level, d):
    return lax.ppermute(x, level[0], shift_perm(level, d))


def take(x, index):
    return lax.dynamic_index_in_dim(x, index, axis=0, keepdims=False)


def softmax_scatter(level, packed):
    size = level[2]
    c = coord(level)
    parts = [take(packed, c)]
    for d in range(1, size):
        parts.append(shifted(take(packed, (c + d) % size), level, d))
    head_dim = packed.shape[-1] - 2
    top_all = parts[0][..., head_dim]
    for p in parts[1:]:
        top_all = jnp.maximum(top_all, p[..., head_dim])
    total_all = 0.0
    mixed_all = 0.0
    for p in parts:
        factor = jnp.exp(p[..., head_dim] - top_all)
        total_all = total_all + p[..., head_dim + 1] * factor
        mixed_all = mixed_all + p[..., :head_dim] * factor[..., None]
    return jnp.concatenate([mixed_all, top_all[..., None], total_all[..., None]], axis=-1)


def sum_scatter_abs(x, level):
    size = level[2]
    c = coord(level)
    acc = take(x, c)
    for d in range(1, size):
        acc = acc + shifted(take(x, (c + d) % size), level, d)
    return acc


def sum_all_ordered(x, level):
    size = level[2]
    c = coord(level)
    parts = [x] + [shifted(x, level, d) for d in range(1, size)]
    total = None
    for m in range(size):
        part = parts[0]
        for d in range(1, size):
            part = jnp.where((c - d) % size == m, parts[d], part)
        total = part if total is None else total + part
    return total


def gather_rel(x, level):
    size = level[2]
    parts = [x] + [shifted(x, level, d) for d in range(1, size)]
    return jnp.stack(parts, axis=0)


def sum_scatter_rel(x, level, wire):
    size = level[2]
    acc = x[0]
    for d in range(1, size):
        acc = acc + shifted(x[size - d].astype(wire), level, d).astype(acc.dtype)
    return acc


def rms_norm(values, gain_vector):
    floats = values.astype(jnp.float32)
    square_mean = jnp.mean(floats * floats, axis=-1, keepdims=True)
    return (floats * lax.rsqrt(square_mean + norm_eps) * gain_vector.astype(jnp.float32)).astype(
        jnp.bfloat16
    )


def rotate(vectors, positions):
    half_size = vectors.shape[-1] // 2
    inverse = jnp.exp(
        jnp.arange(half_size, dtype=jnp.float32) * (-2.0 * math.log(rope_theta) / vectors.shape[-1])
    )
    angles = positions.astype(jnp.float32)[..., None] * inverse
    cosine = jnp.cos(angles)[..., None, :]
    sine = jnp.sin(angles)[..., None, :]
    first_half = vectors[..., :half_size]
    second_half = vectors[..., half_size:]
    return jnp.concatenate(
        [first_half * cosine - second_half * sine, second_half * cosine + first_half * sine],
        axis=-1,
    )


BLOCK_REQ = 16


def cache_kernel(start_ref, len_ref, q_ref, k_ref, v_ref, packed_ref):
    block = pl.program_id(0)
    rows = q_ref.shape[1]
    half = rows // 2
    head_dim = packed_ref.shape[2] - 2
    shard_len = k_ref.shape[1]
    slots = lax.broadcasted_iota(jnp.int32, (1, shard_len), 1)
    for i in range(q_ref.shape[0]):
        r = block * q_ref.shape[0] + i
        rel = slots + start_ref[r]
        rel = jnp.where(rel >= S_CAP, rel - S_CAP, rel)
        live = rel < len_ref[r]
        scores = lax.dot_general(q_ref[i], k_ref[i], (((1,), (1,)), ((), ())),
                                 preferred_element_type=jnp.float32) * attn_scale
        top = jnp.max(jnp.where(live, scores, neg_large), axis=-1, keepdims=True)
        weights = jnp.where(live, jnp.exp(scores - top), 0.0)
        packed_ref[i, :, head_dim:head_dim + 1] = top
        packed_ref[i, :, head_dim + 1:head_dim + 2] = jnp.sum(weights, axis=-1, keepdims=True)
        mixed = jnp.dot(weights.astype(jnp.bfloat16), v_ref[i], preferred_element_type=jnp.float32)
        packed_ref[i, 0:half, 0:head_dim] = mixed[0:half, 0:head_dim]
        packed_ref[i, half:rows, 0:head_dim] = mixed[half:rows, head_dim:2 * head_dim]


def cache_attention(start, lengths, spread, keys, values, head_dim):
    req, rows, width = spread.shape
    shard_len = keys.shape[1]
    grid = (req // BLOCK_REQ,)
    def blk(b, s, l):
        return (b, 0, 0)
    return pl.pallas_call(
        cache_kernel,
        out_shape=jax.ShapeDtypeStruct((req, rows, head_dim + 2), jnp.float32),
        grid_spec=pltpu.PrefetchScalarGridSpec(
            num_scalar_prefetch=2, grid=grid,
            in_specs=[pl.BlockSpec((BLOCK_REQ, rows, width), blk),
                      pl.BlockSpec((BLOCK_REQ, shard_len, width), blk),
                      pl.BlockSpec((BLOCK_REQ, shard_len, width), blk)],
            out_specs=pl.BlockSpec((BLOCK_REQ, rows, head_dim + 2), blk)),
    )(start, lengths, spread, keys, values)


def attend_shard(query_sel, keys_sel, values_sel, lengths_sel, offsets_sel, slot_base):
    step_count, request_count, local_kv, group_size, head_dim = query_sel.shape
    query_rows = jnp.transpose(query_sel, (1, 2, 0, 3, 4)).reshape(
        request_count, local_kv, step_count * group_size, head_dim
    )
    blank = jnp.zeros((request_count, step_count * group_size, head_dim), query_sel.dtype)
    spread = jnp.concatenate(
        [
            jnp.concatenate([query_rows[:, k] if j == k else blank for j in range(local_kv)], axis=-1)
            for k in range(local_kv)
        ],
        axis=1,
    )
    start = (slot_base - offsets_sel) % S_CAP
    return cache_attention(start, lengths_sel, spread, keys_sel, values_sel, head_dim)


def local(
    hidden_in,
    lengths,
    request_perm,
    k_cache,
    v_cache,
    attn_gain,
    w_query,
    w_key,
    w_value,
    w_out,
    mlp_gain,
    w_gate,
    w_up,
    w_down,
):
    step_count, request_count, model_width = hidden_in.shape
    row_total = step_count * request_count
    group_size = H // KVH
    local_kv = k_cache.shape[2] // HD
    local_heads = local_kv * group_size
    shard_len = k_cache.shape[1]
    flat_in = hidden_in.reshape(row_total, model_width)
    normed = rms_norm(flat_in, attn_gain)
    positions = lengths[None, :] + jnp.arange(step_count, dtype=jnp.int32)[:, None]
    query_raw = jnp.dot(normed, w_query, preferred_element_type=jnp.float32).reshape(
        step_count, request_count, local_heads, HD
    )
    key_raw = jnp.dot(normed, w_key, preferred_element_type=jnp.float32).reshape(
        step_count, request_count, local_kv, HD
    )
    value_new = (
        jnp.dot(normed, w_value, preferred_element_type=jnp.float32)
        .astype(jnp.bfloat16)
        .reshape(step_count, request_count, local_kv, HD)
    )
    queries = (
        rotate(query_raw, positions)
        .astype(jnp.bfloat16)
        .reshape(step_count, request_count, local_kv, group_size, HD)
    )
    key_new = rotate(key_raw, positions).astype(jnp.bfloat16)
    offsets = request_perm * S_CAP // request_count
    slot_base = lax.axis_index("seq") * shard_len
    packed = attend_shard(queries, k_cache, v_cache, lengths, offsets, slot_base)

    levels = (CORE, ZAX, XAX)
    packed = packed.reshape((2, 4, 4, -1) + packed.shape[1:])
    for level in levels:
        packed = softmax_scatter(level, packed)
    own_shape = (packed.shape[0], local_kv, step_count, group_size)
    top_s = packed[..., HD].reshape(own_shape)
    total_s = packed[..., HD + 1].reshape(own_shape)
    mixed_s = packed[..., :HD].reshape(own_shape + (HD,))
    own_count = top_s.shape[0]
    first_req = ((coord(CORE) * 4 + coord(ZAX)) * 4 + coord(XAX)) * own_count

    def own(x):
        return lax.dynamic_slice_in_dim(x, first_req, own_count, axis=1)

    queries_own = own(queries)
    key_own = own(key_new)
    value_own = own(value_new)
    causal = jnp.arange(step_count)[None, :] <= jnp.arange(step_count)[:, None]
    causal_full = causal[None, None, :, None, :]
    new_scores = (
        jnp.einsum("trkgd,urkd->rktgu", queries_own, key_own, preferred_element_type=jnp.float32)
        * attn_scale
    )
    top_new = jnp.max(jnp.where(causal_full, new_scores, neg_large), axis=-1)
    top_final = jnp.maximum(top_s, top_new)
    new_weights = jnp.where(causal_full, jnp.exp(new_scores - top_final[..., None]), 0.0)
    new_mixed = jnp.einsum(
        "rktgu,urkd->rktgd",
        new_weights.astype(jnp.bfloat16),
        value_own,
        preferred_element_type=jnp.float32,
    )
    weight_cache = jnp.exp(top_s - top_final)
    denominator = total_s * weight_cache + jnp.sum(new_weights, axis=-1)
    heads = (mixed_s * weight_cache[..., None] + new_mixed) / denominator[..., None]
    heads = (
        jnp.transpose(heads, (2, 0, 1, 3, 4))
        .reshape(step_count * own_count, local_heads * HD)
        .astype(jnp.bfloat16)
    )
    attended_part = jnp.dot(heads, w_out, preferred_element_type=jnp.float32).reshape(
        step_count, own_count, model_width
    )
    attended = sum_all_ordered(attended_part.reshape(-1, model_width), YAX)
    hidden_own = lax.dynamic_slice_in_dim(hidden_in, first_req, own_count, axis=1).reshape(
        -1, model_width
    )
    residual = (hidden_own.astype(jnp.float32) + branch_scale * attended).astype(jnp.bfloat16)
    normed_mlp = rms_norm(residual, mlp_gain)

    gather_levels = (XAX, ZAX)
    rows = normed_mlp
    for level in gather_levels:
        rows = gather_rel(rows, level)
    halves = (rows, shifted(rows, CORE, 1))
    block_shape = rows.shape[:-1]
    contract_rows = (((1,), (1,)), ((), ()))

    def feed(half_rows):
        flat = half_rows.reshape(-1, model_width)
        gate = lax.dot_general(flat, w_gate, contract_rows, preferred_element_type=jnp.float32)
        up_proj = lax.dot_general(flat, w_up, contract_rows, preferred_element_type=jnp.float32)
        hidden = (jax.nn.silu(gate) * up_proj).astype(jnp.bfloat16)
        return jnp.dot(hidden, w_down, preferred_element_type=jnp.float32).reshape(
            block_shape + (model_width,)
        )

    feed_forward = feed(halves[0]) + shifted(feed(halves[1]), CORE, 1)
    for level in reversed(gather_levels):
        feed_forward = sum_scatter_rel(feed_forward, level, jnp.bfloat16)
    feed_forward = sum_all_ordered(feed_forward, YAX)
    output = (residual.astype(jnp.float32) + branch_scale * feed_forward).astype(jnp.bfloat16)

    out_rows = output
    for level in gather_levels:
        out_rows = gather_rel(out_rows, level)
    out_halves = (out_rows, shifted(out_rows, CORE, 1))
    own_rows = out_rows.shape[2]
    half_flat = [h.reshape(-1, model_width) for h in out_halves]
    half_count = half_flat[0].shape[0]
    dest = jnp.arange(2 * half_count, dtype=jnp.int32)
    pair = dest % own_count
    dest = dest // own_count
    member = {}
    for level in (XAX, ZAX, CORE):
        member[level] = dest % level[2]
        dest = dest // level[2]
    step_of = dest % step_count
    source = jnp.zeros_like(dest)
    for level in (CORE, ZAX, XAX):
        size = level[2]
        source = source * size + (coord(level) - member[level]) % size
    source = source * own_rows + step_of * own_count + pair
    merged = 0.0
    for kc, flat in enumerate(half_flat):
        cols = kc * half_count + jnp.arange(half_count, dtype=jnp.int32)
        one_hot = (source[:, None] == cols[None, :]).astype(flat.dtype)
        merged = merged + jnp.dot(one_hot, flat, preferred_element_type=jnp.float32)
    hidden_out = merged.astype(jnp.bfloat16).reshape(step_count, request_count, model_width)
    key_out = key_new.reshape(step_count, request_count, local_kv * HD)
    value_out = value_new.reshape(step_count, request_count, local_kv * HD)
    return (hidden_out, key_out, value_out)


def solution(mesh):
    placed = (
        P(),
        P(),
        P(),
        P(None, "seq", "tp"),
        P(None, "seq", "tp"),
        P(),
        P(None, "tp"),
        P(None, "tp"),
        P(None, "tp"),
        P("tp", None),
        P(),
        P(("seq", "tp"), None),
        P(("seq", "tp"), None),
        P(("seq", "tp"), None),
    )
    return jax.shard_map(
        local,
        mesh=mesh,
        in_specs=placed,
        out_specs=(P(), P(None, None, "tp"), P(None, None, "tp")),
        check_vma=False,
    )
```

```python
import math

import jax
import jax.numpy as jnp
from jax import lax
from jax.experimental import pallas as pl
from jax.experimental.pallas import tpu as pltpu
from jax.sharding import PartitionSpec as P

H = 32
KVH = 8
HD = 64
S_CAP = 16384


norm_eps = 1e-05
rope_theta = 10000000.0
attn_scale = 0.015625
branch_scale = 0.5
neg_large = -1e30

CORE = ("seq", 1, 2)
ZAX = ("seq", 2, 4)
XAX = ("seq", 8, 4)
YAX = ("tp", 1, 4)
AXIS_SIZE = {"seq": 32, "tp": 4}


def coord(level):
    axis, stride, size = level
    return (lax.axis_index(axis) // stride) % size


def shift_perm(level, d):
    axis, stride, size = level
    pairs = []
    for i in range(AXIS_SIZE[axis]):
        c = (i // stride) % size
        pairs.append((i, i + ((c + d) % size - c) * stride))
    return pairs


def shifted(x, level, d):
    return lax.ppermute(x, level[0], shift_perm(level, d))


def take(x, index):
    return lax.dynamic_index_in_dim(x, index, axis=0, keepdims=False)


def softmax_scatter(level, packed):
    size = level[2]
    c = coord(level)
    parts = [take(packed, c)]
    for d in range(1, size):
        parts.append(shifted(take(packed, (c + d) % size), level, d))
    head_dim = packed.shape[-1] - 2
    top_all = parts[0][..., head_dim]
    for p in parts[1:]:
        top_all = jnp.maximum(top_all, p[..., head_dim])
    total_all = 0.0
    mixed_all = 0.0
    for p in parts:
        factor = jnp.exp(p[..., head_dim] - top_all)
        total_all = total_all + p[..., head_dim + 1] * factor
        mixed_all = mixed_all + p[..., :head_dim] * factor[..., None]
    return jnp.concatenate([mixed_all, top_all[..., None], total_all[..., None]], axis=-1)


def sum_all_ordered(x, level):
    size = level[2]
    c = coord(level)
    parts = [x] + [shifted(x, level, d) for d in range(1, size)]
    total = None
    for m in range(size):
        part = parts[0]
        for d in range(1, size):
            part = jnp.where((c - d) % size == m, parts[d], part)
        total = part if total is None else total + part
    return total


def gather_rel(x, level):
    size = level[2]
    parts = [x] + [shifted(x, level, d) for d in range(1, size)]
    return jnp.stack(parts, axis=0)


def sum_scatter_rel(x, level, wire):
    size = level[2]
    acc = x[0]
    for d in range(1, size):
        acc = acc + shifted(x[size - d].astype(wire), level, d).astype(acc.dtype)
    return acc


def rms_norm(values, gain_vector):
    floats = values.astype(jnp.float32)
    square_mean = jnp.mean(floats * floats, axis=-1, keepdims=True)
    return (floats * lax.rsqrt(square_mean + norm_eps) * gain_vector.astype(jnp.float32)).astype(
        jnp.bfloat16
    )


def rotate(vectors, positions):
    half_size = vectors.shape[-1] // 2
    inverse = jnp.exp(
        jnp.arange(half_size, dtype=jnp.float32) * (-2.0 * math.log(rope_theta) / vectors.shape[-1])
    )
    angles = positions.astype(jnp.float32)[..., None] * inverse
    cosine = jnp.cos(angles)[..., None, :]
    sine = jnp.sin(angles)[..., None, :]
    first_half = vectors[..., :half_size]
    second_half = vectors[..., half_size:]
    return jnp.concatenate(
        [first_half * cosine - second_half * sine, second_half * cosine + first_half * sine],
        axis=-1,
    )


BLOCK_REQ = 16


def cache_kernel(start_ref, len_ref, q_ref, k_ref, v_ref, packed_ref):
    block = pl.program_id(0)
    rows = q_ref.shape[1]
    half = rows // 2
    head_dim = packed_ref.shape[2] - 2
    shard_len = k_ref.shape[1]
    slots = lax.broadcasted_iota(jnp.int32, (1, shard_len), 1)
    for i in range(q_ref.shape[0]):
        r = block * q_ref.shape[0] + i
        rel = slots + start_ref[r]
        rel = jnp.where(rel >= S_CAP, rel - S_CAP, rel)
        live = rel < len_ref[r]
        scores = lax.dot_general(q_ref[i], k_ref[i], (((1,), (1,)), ((), ())),
                                 preferred_element_type=jnp.float32) * attn_scale
        top = jnp.max(jnp.where(live, scores, neg_large), axis=-1, keepdims=True)
        weights = jnp.where(live, jnp.exp(scores - top), 0.0)
        packed_ref[i, :, head_dim:head_dim + 1] = top
        packed_ref[i, :, head_dim + 1:head_dim + 2] = jnp.sum(weights, axis=-1, keepdims=True)
        mixed = jnp.dot(weights.astype(jnp.bfloat16), v_ref[i], preferred_element_type=jnp.float32)
        packed_ref[i, 0:half, 0:head_dim] = mixed[0:half, 0:head_dim]
        packed_ref[i, half:rows, 0:head_dim] = mixed[half:rows, head_dim:2 * head_dim]


def cache_attention(start, lengths, spread, keys, values, head_dim):
    req, rows, width = spread.shape
    shard_len = keys.shape[1]
    grid = (req // BLOCK_REQ,)

    def blk(b, s, l):
        return (b, 0, 0)

    return pl.pallas_call(
        cache_kernel,
        out_shape=jax.ShapeDtypeStruct((req, rows, head_dim + 2), jnp.float32),
        grid_spec=pltpu.PrefetchScalarGridSpec(
            num_scalar_prefetch=2, grid=grid,
            in_specs=[pl.BlockSpec((BLOCK_REQ, rows, width), blk),
                      pl.BlockSpec((BLOCK_REQ, shard_len, width), blk),
                      pl.BlockSpec((BLOCK_REQ, shard_len, width), blk)],
            out_specs=pl.BlockSpec((BLOCK_REQ, rows, head_dim + 2), blk)),
    )(start, lengths, spread, keys, values)


def attend_shard(query_sel, keys_sel, values_sel, lengths_sel, offsets_sel, slot_base):
    step_count, request_count, local_kv, group_size, head_dim = query_sel.shape
    query_rows = jnp.transpose(query_sel, (1, 2, 0, 3, 4)).reshape(
        request_count, local_kv, step_count * group_size, head_dim
    )
    blank = jnp.zeros((request_count, step_count * group_size, head_dim), query_sel.dtype)
    spread = jnp.concatenate(
        [
            jnp.concatenate([query_rows[:, k] if j == k else blank for j in range(local_kv)], axis=-1)
            for k in range(local_kv)
        ],
        axis=1,
    )
    start = (slot_base - offsets_sel) % S_CAP
    return cache_attention(start, lengths_sel, spread, keys_sel, values_sel, head_dim)


def local_body(
    hidden_in,
    lengths,
    request_perm,
    k_cache,
    v_cache,
    attn_gain,
    w_query,
    w_key,
    w_value,
    w_out,
    mlp_gain,
    w_gate,
    w_up,
    w_down,
):
    step_count, request_count, model_width = hidden_in.shape
    row_total = step_count * request_count
    group_size = H // KVH
    local_kv = k_cache.shape[2] // HD
    local_heads = local_kv * group_size
    shard_len = k_cache.shape[1]
    flat_in = hidden_in.reshape(row_total, model_width)
    normed = rms_norm(flat_in, attn_gain)
    positions = lengths[None, :] + jnp.arange(step_count, dtype=jnp.int32)[:, None]
    query_raw = jnp.dot(normed, w_query, preferred_element_type=jnp.float32).reshape(
        step_count, request_count, local_heads, HD
    )
    queries = (
        rotate(query_raw, positions)
        .astype(jnp.bfloat16)
        .reshape(step_count, request_count, local_kv, group_size, HD)
    )
    offsets = request_perm * S_CAP // request_count
    slot_base = lax.axis_index("seq") * shard_len
    packed = attend_shard(queries, k_cache, v_cache, lengths, offsets, slot_base)

    own_count = request_count // (2 * 4 * 4)
    first_req = ((coord(CORE) * 4 + coord(ZAX)) * 4 + coord(XAX)) * own_count

    def own(x):
        return lax.dynamic_slice_in_dim(x, first_req, own_count, axis=1)

    key_raw = jnp.dot(normed, w_key, preferred_element_type=jnp.float32).reshape(
        step_count, request_count, local_kv, HD
    )
    value_new = (
        jnp.dot(normed, w_value, preferred_element_type=jnp.float32)
        .astype(jnp.bfloat16)
        .reshape(step_count, request_count, local_kv, HD)
    )
    key_new = rotate(key_raw, positions).astype(jnp.bfloat16)
    queries_own = own(queries)
    key_own = own(key_new)
    value_own = own(value_new)
    causal = jnp.arange(step_count)[None, :] <= jnp.arange(step_count)[:, None]
    causal_full = causal[None, None, :, None, :]
    new_scores = (
        jnp.einsum("trkgd,urkd->rktgu", queries_own, key_own, preferred_element_type=jnp.float32)
        * attn_scale
    )
    top_new = jnp.max(jnp.where(causal_full, new_scores, neg_large), axis=-1)

    levels = (CORE, ZAX, XAX)
    packed = packed.reshape((2, 4, 4, -1) + packed.shape[1:])
    for level in levels:
        packed = softmax_scatter(level, packed)
    own_shape = (packed.shape[0], local_kv, step_count, group_size)
    top_s = packed[..., HD].reshape(own_shape)
    total_s = packed[..., HD + 1].reshape(own_shape)
    mixed_s = packed[..., :HD].reshape(own_shape + (HD,))
    top_final = jnp.maximum(top_s, top_new)
    new_weights = jnp.where(causal_full, jnp.exp(new_scores - top_final[..., None]), 0.0)
    new_mixed = jnp.einsum(
        "rktgu,urkd->rktgd",
        new_weights.astype(jnp.bfloat16),
        value_own,
        preferred_element_type=jnp.float32,
    )
    weight_cache = jnp.exp(top_s - top_final)
    denominator = total_s * weight_cache + jnp.sum(new_weights, axis=-1)
    heads = (mixed_s * weight_cache[..., None] + new_mixed) / denominator[..., None]
    heads = (
        jnp.transpose(heads, (2, 0, 1, 3, 4))
        .reshape(step_count * own_count, local_heads * HD)
        .astype(jnp.bfloat16)
    )
    attended_part = jnp.dot(heads, w_out, preferred_element_type=jnp.float32).reshape(
        step_count, own_count, model_width
    )
    attended = sum_all_ordered(attended_part.reshape(-1, model_width), YAX)
    hidden_own = lax.dynamic_slice_in_dim(hidden_in, first_req, own_count, axis=1).reshape(
        -1, model_width
    )
    residual = (hidden_own.astype(jnp.float32) + branch_scale * attended).astype(jnp.bfloat16)
    normed_mlp = rms_norm(residual, mlp_gain)

    gather_levels = (XAX, ZAX)
    rows = normed_mlp
    for level in gather_levels:
        rows = gather_rel(rows, level)
    halves = (rows, shifted(rows, CORE, 1))
    block_shape = rows.shape[:-1]
    contract_rows = (((1,), (1,)), ((), ()))

    def feed(half_rows):
        flat = half_rows.reshape(-1, model_width)
        gate = lax.dot_general(flat, w_gate, contract_rows, preferred_element_type=jnp.float32)
        up_proj = lax.dot_general(flat, w_up, contract_rows, preferred_element_type=jnp.float32)
        hidden = (jax.nn.silu(gate) * up_proj).astype(jnp.bfloat16)
        return jnp.dot(hidden, w_down, preferred_element_type=jnp.float32).reshape(
            block_shape + (model_width,)
        )

    feed_forward = feed(halves[0]) + shifted(feed(halves[1]), CORE, 1)
    for level in reversed(gather_levels):
        feed_forward = sum_scatter_rel(feed_forward, level, jnp.bfloat16)
    feed_forward = sum_all_ordered(feed_forward, YAX)
    output = (residual.astype(jnp.float32) + branch_scale * feed_forward).astype(jnp.bfloat16)

    out_rows = output
    for level in gather_levels:
        out_rows = gather_rel(out_rows, level)
    out_halves = (out_rows, shifted(out_rows, CORE, 1))
    own_rows = out_rows.shape[2]
    half_flat = [h.reshape(-1, model_width) for h in out_halves]
    half_count = half_flat[0].shape[0]
    dest = jnp.arange(2 * half_count, dtype=jnp.int32)
    pair = dest % own_count
    dest = dest // own_count
    member = {}
    for level in (XAX, ZAX, CORE):
        member[level] = dest % level[2]
        dest = dest // level[2]
    step_of = dest % step_count
    source = jnp.zeros_like(dest)
    for level in (CORE, ZAX, XAX):
        size = level[2]
        source = source * size + (coord(level) - member[level]) % size
    source = source * own_rows + step_of * own_count + pair
    merged = 0.0
    for kc, flat in enumerate(half_flat):
        cols = kc * half_count + jnp.arange(half_count, dtype=jnp.int32)
        one_hot = (source[:, None] == cols[None, :]).astype(flat.dtype)
        merged = merged + jnp.dot(one_hot, flat, preferred_element_type=jnp.float32)
    hidden_out = merged.astype(jnp.bfloat16).reshape(step_count, request_count, model_width)
    key_out = key_new.reshape(step_count, request_count, local_kv * HD)
    value_out = value_new.reshape(step_count, request_count, local_kv * HD)
    return (hidden_out, key_out, value_out)


def solution(mesh):
    placed = (
        P(),
        P(),
        P(),
        P(None, "seq", "tp"),
        P(None, "seq", "tp"),
        P(),
        P(None, "tp"),
        P(None, "tp"),
        P(None, "tp"),
        P("tp", None),
        P(),
        P(("seq", "tp"), None),
        P(("seq", "tp"), None),
        P(("seq", "tp"), None),
    )
    return jax.shard_map(
        local_body,
        mesh=mesh,
        in_specs=placed,
        out_specs=(P(), P(None, None, "tp"), P(None, None, "tp")),
        check_vma=False,
    )
```

```python
import math

import jax
import jax.numpy as jnp
from jax import lax
from jax.experimental import pallas as pl
from jax.experimental.pallas import tpu as pltpu
from jax.sharding import PartitionSpec as P

H = 32
KVH = 8
HD = 64
S_CAP = 16384


norm_eps = 1e-05
rope_theta = 10000000.0
attn_scale = 0.015625
branch_scale = 0.5
neg_large = -1e30

CORE = ("seq", 1, 2)
ZAX = ("seq", 2, 4)
XAX = ("seq", 8, 4)
YAX = ("tp", 1, 4)
AXIS_SIZE = {"seq": 32, "tp": 4}


def coord(level):
    axis, stride, size = level
    return (lax.axis_index(axis) // stride) % size


def shift_perm(level, d):
    axis, stride, size = level
    pairs = []
    for i in range(AXIS_SIZE[axis]):
        c = (i // stride) % size
        pairs.append((i, i + ((c + d) % size - c) * stride))
    return pairs


def shifted(x, level, d):
    return lax.ppermute(x, level[0], shift_perm(level, d))


def take(x, index):
    return lax.dynamic_index_in_dim(x, index, axis=0, keepdims=False)


def softmax_scatter(level, packed):
    size = level[2]
    c = coord(level)
    parts = [take(packed, c)]
    for d in range(1, size):
        parts.append(shifted(take(packed, (c + d) % size), level, d))
    head_dim = packed.shape[-1] - 2
    top_all = parts[0][..., head_dim]
    for p in parts[1:]:
        top_all = jnp.maximum(top_all, p[..., head_dim])
    total_all = 0.0
    mixed_all = 0.0
    for p in parts:
        factor = jnp.exp(p[..., head_dim] - top_all)
        total_all = total_all + p[..., head_dim + 1] * factor
        mixed_all = mixed_all + p[..., :head_dim] * factor[..., None]
    return jnp.concatenate([mixed_all, top_all[..., None], total_all[..., None]], axis=-1)


def sum_scatter_abs(x, level):
    size = level[2]
    c = coord(level)
    acc = take(x, c)
    for d in range(1, size):
        acc = acc + shifted(take(x, (c + d) % size), level, d)
    return acc


def sum_all_ordered(x, level, wire):
    size = level[2]
    c = coord(level)
    sent = x.astype(wire)
    parts = [sent.astype(x.dtype)] + [
        shifted(sent, level, d).astype(x.dtype) for d in range(1, size)
    ]
    total = None
    for m in range(size):
        part = parts[0]
        for d in range(1, size):
            part = jnp.where((c - d) % size == m, parts[d], part)
        total = part if total is None else total + part
    return total


def gather_rel(x, level):
    size = level[2]
    parts = [x] + [shifted(x, level, d) for d in range(1, size)]
    return jnp.stack(parts, axis=0)


def sum_scatter_rel(x, level, wire):
    size = level[2]
    acc = x[0]
    for d in range(1, size):
        acc = acc + shifted(x[size - d].astype(wire), level, d).astype(acc.dtype)
    return acc


def rms_norm(values, gain_vector):
    floats = values.astype(jnp.float32)
    square_mean = jnp.mean(floats * floats, axis=-1, keepdims=True)
    return (floats * lax.rsqrt(square_mean + norm_eps) * gain_vector.astype(jnp.float32)).astype(
        jnp.bfloat16
    )


def rotate(vectors, positions):
    half_size = vectors.shape[-1] // 2
    inverse = jnp.exp(
        jnp.arange(half_size, dtype=jnp.float32) * (-2.0 * math.log(rope_theta) / vectors.shape[-1])
    )
    angles = positions.astype(jnp.float32)[..., None] * inverse
    cosine = jnp.cos(angles)[..., None, :]
    sine = jnp.sin(angles)[..., None, :]
    first_half = vectors[..., :half_size]
    second_half = vectors[..., half_size:]
    return jnp.concatenate(
        [first_half * cosine - second_half * sine, second_half * cosine + first_half * sine],
        axis=-1,
    )


BLOCK_REQ = 16


def cache_kernel(start_ref, len_ref, q_ref, k_ref, v_ref, packed_ref):
    block = pl.program_id(0)
    rows = q_ref.shape[1]
    half = rows // 2
    head_dim = packed_ref.shape[2] - 2
    shard_len = k_ref.shape[1]
    slots = lax.broadcasted_iota(jnp.int32, (1, shard_len), 1)
    for i in range(q_ref.shape[0]):
        r = block * q_ref.shape[0] + i
        rel = slots + start_ref[r]
        rel = jnp.where(rel >= S_CAP, rel - S_CAP, rel)
        live = rel < len_ref[r]
        scores = lax.dot_general(q_ref[i], k_ref[i], (((1,), (1,)), ((), ())),
                                 preferred_element_type=jnp.float32) * attn_scale
        top = jnp.max(jnp.where(live, scores, neg_large), axis=-1, keepdims=True)
        weights = jnp.where(live, jnp.exp(scores - top), 0.0)
        packed_ref[i, :, head_dim:head_dim + 1] = top
        packed_ref[i, :, head_dim + 1:head_dim + 2] = jnp.sum(weights, axis=-1, keepdims=True)
        mixed = jnp.dot(weights.astype(jnp.bfloat16), v_ref[i], preferred_element_type=jnp.float32)
        packed_ref[i, 0:half, 0:head_dim] = mixed[0:half, 0:head_dim]
        packed_ref[i, half:rows, 0:head_dim] = mixed[half:rows, head_dim:2 * head_dim]


def cache_attention(start, lengths, spread, keys, values, head_dim):
    req, rows, width = spread.shape
    shard_len = keys.shape[1]
    grid = (req // BLOCK_REQ,)
    def blk(b, s, l):
        return (b, 0, 0)
    return pl.pallas_call(
        cache_kernel,
        out_shape=jax.ShapeDtypeStruct((req, rows, head_dim + 2), jnp.float32),
        grid_spec=pltpu.PrefetchScalarGridSpec(
            num_scalar_prefetch=2, grid=grid,
            in_specs=[pl.BlockSpec((BLOCK_REQ, rows, width), blk),
                      pl.BlockSpec((BLOCK_REQ, shard_len, width), blk),
                      pl.BlockSpec((BLOCK_REQ, shard_len, width), blk)],
            out_specs=pl.BlockSpec((BLOCK_REQ, rows, head_dim + 2), blk)),
    )(start, lengths, spread, keys, values)


def attend_shard(query_sel, keys_sel, values_sel, lengths_sel, offsets_sel, slot_base):
    step_count, request_count, local_kv, group_size, head_dim = query_sel.shape
    query_rows = jnp.transpose(query_sel, (1, 2, 0, 3, 4)).reshape(
        request_count, local_kv, step_count * group_size, head_dim
    )
    blank = jnp.zeros((request_count, step_count * group_size, head_dim), query_sel.dtype)
    spread = jnp.concatenate(
        [
            jnp.concatenate([query_rows[:, k] if j == k else blank for j in range(local_kv)], axis=-1)
            for k in range(local_kv)
        ],
        axis=1,
    )
    start = (slot_base - offsets_sel) % S_CAP
    return cache_attention(start, lengths_sel, spread, keys_sel, values_sel, head_dim)


def local(
    hidden_in,
    lengths,
    request_perm,
    k_cache,
    v_cache,
    attn_gain,
    w_query,
    w_key,
    w_value,
    w_out,
    mlp_gain,
    w_gate,
    w_up,
    w_down,
):
    step_count, request_count, model_width = hidden_in.shape
    row_total = step_count * request_count
    group_size = H // KVH
    local_kv = k_cache.shape[2] // HD
    local_heads = local_kv * group_size
    shard_len = k_cache.shape[1]
    flat_in = hidden_in.reshape(row_total, model_width)
    normed = rms_norm(flat_in, attn_gain)
    positions = lengths[None, :] + jnp.arange(step_count, dtype=jnp.int32)[:, None]
    query_raw = jnp.dot(normed, w_query, preferred_element_type=jnp.float32).reshape(
        step_count, request_count, local_heads, HD
    )
    key_raw = jnp.dot(normed, w_key, preferred_element_type=jnp.float32).reshape(
        step_count, request_count, local_kv, HD
    )
    value_new = (
        jnp.dot(normed, w_value, preferred_element_type=jnp.float32)
        .astype(jnp.bfloat16)
        .reshape(step_count, request_count, local_kv, HD)
    )
    queries = (
        rotate(query_raw, positions)
        .astype(jnp.bfloat16)
        .reshape(step_count, request_count, local_kv, group_size, HD)
    )
    key_new = rotate(key_raw, positions).astype(jnp.bfloat16)
    offsets = request_perm * S_CAP // request_count
    slot_base = lax.axis_index("seq") * shard_len
    packed = attend_shard(queries, k_cache, v_cache, lengths, offsets, slot_base)

    levels = (CORE, ZAX, XAX)
    packed = packed.reshape((2, 4, 4, -1) + packed.shape[1:])
    for level in levels:
        packed = softmax_scatter(level, packed)
    own_shape = (packed.shape[0], local_kv, step_count, group_size)
    top_s = packed[..., HD].reshape(own_shape)
    total_s = packed[..., HD + 1].reshape(own_shape)
    mixed_s = packed[..., :HD].reshape(own_shape + (HD,))
    own_count = top_s.shape[0]
    first_req = ((coord(CORE) * 4 + coord(ZAX)) * 4 + coord(XAX)) * own_count

    def own(x):
        return lax.dynamic_slice_in_dim(x, first_req, own_count, axis=1)

    queries_own = own(queries)
    key_own = own(key_new)
    value_own = own(value_new)
    causal = jnp.arange(step_count)[None, :] <= jnp.arange(step_count)[:, None]
    causal_full = causal[None, None, :, None, :]
    new_scores = (
        jnp.einsum("trkgd,urkd->rktgu", queries_own, key_own, preferred_element_type=jnp.float32)
        * attn_scale
    )
    top_new = jnp.max(jnp.where(causal_full, new_scores, neg_large), axis=-1)
    top_final = jnp.maximum(top_s, top_new)
    new_weights = jnp.where(causal_full, jnp.exp(new_scores - top_final[..., None]), 0.0)
    new_mixed = jnp.einsum(
        "rktgu,urkd->rktgd",
        new_weights.astype(jnp.bfloat16),
        value_own,
        preferred_element_type=jnp.float32,
    )
    weight_cache = jnp.exp(top_s - top_final)
    denominator = total_s * weight_cache + jnp.sum(new_weights, axis=-1)
    heads = (mixed_s * weight_cache[..., None] + new_mixed) / denominator[..., None]
    heads = (
        jnp.transpose(heads, (2, 0, 1, 3, 4))
        .reshape(step_count * own_count, local_heads * HD)
        .astype(jnp.bfloat16)
    )
    attended_part = jnp.dot(heads, w_out, preferred_element_type=jnp.float32).reshape(
        step_count, own_count, model_width
    )
    attended = sum_all_ordered(attended_part.reshape(-1, model_width), YAX, jnp.float32)
    hidden_own = lax.dynamic_slice_in_dim(hidden_in, first_req, own_count, axis=1).reshape(
        -1, model_width
    )
    residual = (hidden_own.astype(jnp.float32) + branch_scale * attended).astype(jnp.bfloat16)
    normed_mlp = rms_norm(residual, mlp_gain)

    gather_levels = (XAX, ZAX)
    rows = normed_mlp
    for level in gather_levels:
        rows = gather_rel(rows, level)
    halves = (rows, shifted(rows, CORE, 1))
    block_shape = rows.shape[:-1]
    contract_rows = (((1,), (1,)), ((), ()))

    def feed(half_rows):
        flat = half_rows.reshape(-1, model_width)
        gate = lax.dot_general(flat, w_gate, contract_rows, preferred_element_type=jnp.float32)
        up_proj = lax.dot_general(flat, w_up, contract_rows, preferred_element_type=jnp.float32)
        hidden = (jax.nn.silu(gate) * up_proj).astype(jnp.bfloat16)
        return jnp.dot(hidden, w_down, preferred_element_type=jnp.float32).reshape(
            block_shape + (model_width,)
        )

    feed_forward = feed(halves[0]) + shifted(
        feed(halves[1]).astype(jnp.bfloat16), CORE, 1
    ).astype(jnp.float32)
    for level in reversed(gather_levels):
        feed_forward = sum_scatter_rel(feed_forward, level, jnp.bfloat16)
    feed_forward = sum_all_ordered(feed_forward, YAX, jnp.bfloat16)
    output = (residual.astype(jnp.float32) + branch_scale * feed_forward).astype(jnp.bfloat16)

    out_rows = output
    for level in gather_levels:
        out_rows = gather_rel(out_rows, level)
    out_halves = (out_rows, shifted(out_rows, CORE, 1))
    own_rows = out_rows.shape[2]
    half_flat = [h.reshape(-1, model_width) for h in out_halves]
    half_count = half_flat[0].shape[0]
    dest = jnp.arange(2 * half_count, dtype=jnp.int32)
    pair = dest % own_count
    dest = dest // own_count
    member = {}
    for level in (XAX, ZAX, CORE):
        member[level] = dest % level[2]
        dest = dest // level[2]
    step_of = dest % step_count
    source = jnp.zeros_like(dest)
    for level in (CORE, ZAX, XAX):
        size = level[2]
        source = source * size + (coord(level) - member[level]) % size
    source = source * own_rows + step_of * own_count + pair
    merged = 0.0
    for kc, flat in enumerate(half_flat):
        cols = kc * half_count + jnp.arange(half_count, dtype=jnp.int32)
        one_hot = (source[:, None] == cols[None, :]).astype(flat.dtype)
        merged = merged + jnp.dot(one_hot, flat, preferred_element_type=jnp.float32)
    hidden_out = merged.astype(jnp.bfloat16).reshape(step_count, request_count, model_width)
    key_out = key_new.reshape(step_count, request_count, local_kv * HD)
    value_out = value_new.reshape(step_count, request_count, local_kv * HD)
    return (hidden_out, key_out, value_out)


def solution(mesh):
    placed = (
        P(),
        P(),
        P(),
        P(None, "seq", "tp"),
        P(None, "seq", "tp"),
        P(),
        P(None, "tp"),
        P(None, "tp"),
        P(None, "tp"),
        P("tp", None),
        P(),
        P(("seq", "tp"), None),
        P(("seq", "tp"), None),
        P(("seq", "tp"), None),
    )
    return jax.shard_map(
        local,
        mesh=mesh,
        in_specs=placed,
        out_specs=(P(), P(None, None, "tp"), P(None, None, "tp")),
        check_vma=False,
    )
```

```python
import math

import jax
import jax.numpy as jnp
from jax import lax
from jax.experimental import pallas as pl
from jax.experimental.pallas import tpu as pltpu
from jax.sharding import PartitionSpec as P

H = 32
KVH = 8
HD = 64
S_CAP = 16384


norm_eps = 1e-05
rope_theta = 10000000.0
attn_scale = 0.015625
branch_scale = 0.5
neg_large = -1e30

CORE = ("seq", 1, 2)
ZAX = ("seq", 2, 4)
XAX = ("seq", 8, 4)
YAX = ("tp", 1, 4)
AXIS_SIZE = {"seq": 32, "tp": 4}


def coord(level):
    axis, stride, size = level
    return (lax.axis_index(axis) // stride) % size


def shift_perm(level, d):
    axis, stride, size = level
    pairs = []
    for i in range(AXIS_SIZE[axis]):
        c = (i // stride) % size
        pairs.append((i, i + ((c + d) % size - c) * stride))
    return pairs


def shifted(x, level, d):
    return lax.ppermute(x, level[0], shift_perm(level, d))


def take(x, index):
    return lax.dynamic_index_in_dim(x, index, axis=0, keepdims=False)


def softmax_scatter(level, packed):
    size = level[2]
    c = coord(level)
    parts = [take(packed, c)]
    for d in range(1, size):
        parts.append(shifted(take(packed, (c + d) % size), level, d))
    head_dim = packed.shape[-1] - 2
    top_all = parts[0][..., head_dim]
    for p in parts[1:]:
        top_all = jnp.maximum(top_all, p[..., head_dim])
    total_all = 0.0
    mixed_all = 0.0
    for p in parts:
        factor = jnp.exp(p[..., head_dim] - top_all)
        total_all = total_all + p[..., head_dim + 1] * factor
        mixed_all = mixed_all + p[..., :head_dim] * factor[..., None]
    return jnp.concatenate([mixed_all, top_all[..., None], total_all[..., None]], axis=-1)


def sum_scatter_abs(x, level):
    size = level[2]
    c = coord(level)
    acc = take(x, c)
    for d in range(1, size):
        acc = acc + shifted(take(x, (c + d) % size), level, d)
    return acc


def sum_all_ordered(x, level):
    size = level[2]
    c = coord(level)
    parts = [x] + [shifted(x, level, d) for d in range(1, size)]
    total = None
    for m in range(size):
        part = parts[0]
        for d in range(1, size):
            part = jnp.where((c - d) % size == m, parts[d], part)
        total = part if total is None else total + part
    return total


def gather_rel(x, level):
    size = level[2]
    parts = [x] + [shifted(x, level, d) for d in range(1, size)]
    return jnp.stack(parts, axis=0)


def sum_scatter_rel(x, level, wire):
    size = level[2]
    acc = x[0]
    for d in range(1, size):
        acc = acc + shifted(x[size - d].astype(wire), level, d).astype(acc.dtype)
    return acc


def rms_norm(values, gain_vector):
    floats = values.astype(jnp.float32)
    square_mean = jnp.mean(floats * floats, axis=-1, keepdims=True)
    return (floats * lax.rsqrt(square_mean + norm_eps) * gain_vector.astype(jnp.float32)).astype(
        jnp.bfloat16
    )


def rotate(vectors, positions):
    half_size = vectors.shape[-1] // 2
    inverse = jnp.exp(
        jnp.arange(half_size, dtype=jnp.float32) * (-2.0 * math.log(rope_theta) / vectors.shape[-1])
    )
    angles = positions.astype(jnp.float32)[..., None] * inverse
    cosine = jnp.cos(angles)[..., None, :]
    sine = jnp.sin(angles)[..., None, :]
    first_half = vectors[..., :half_size]
    second_half = vectors[..., half_size:]
    return jnp.concatenate(
        [first_half * cosine - second_half * sine, second_half * cosine + first_half * sine],
        axis=-1,
    )


BLOCK_REQ = 16


def cache_kernel(start_ref, len_ref, q_ref, k_ref, v_ref, packed_ref):
    block = pl.program_id(0)
    rows = q_ref.shape[1]
    half = rows // 2
    head_dim = packed_ref.shape[2] - 2
    shard_len = k_ref.shape[1]
    slots = lax.broadcasted_iota(jnp.int32, (1, shard_len), 1)
    for i in range(q_ref.shape[0]):
        r = block * q_ref.shape[0] + i
        rel = slots + start_ref[r]
        rel = jnp.where(rel >= S_CAP, rel - S_CAP, rel)
        live = rel < len_ref[r]
        scores = lax.dot_general(q_ref[i], k_ref[i], (((1,), (1,)), ((), ())),
                                 preferred_element_type=jnp.float32) * attn_scale
        top = jnp.max(jnp.where(live, scores, neg_large), axis=-1, keepdims=True)
        weights = jnp.where(live, jnp.exp(scores - top), 0.0)
        packed_ref[i, :, head_dim:head_dim + 2] = jnp.concatenate(
            [top, jnp.sum(weights, axis=-1, keepdims=True)], axis=-1
        )
        mixed = jnp.dot(weights.astype(jnp.bfloat16), v_ref[i], preferred_element_type=jnp.float32)
        packed_ref[i, 0:half, 0:head_dim] = mixed[0:half, 0:head_dim]
        packed_ref[i, half:rows, 0:head_dim] = mixed[half:rows, head_dim:2 * head_dim]


def cache_attention(start, lengths, spread, keys, values, head_dim):
    req, rows, width = spread.shape
    shard_len = keys.shape[1]
    grid = (req // BLOCK_REQ,)
    def blk(b, s, l):
        return (b, 0, 0)
    return pl.pallas_call(
        cache_kernel,
        out_shape=jax.ShapeDtypeStruct((req, rows, head_dim + 2), jnp.float32),
        grid_spec=pltpu.PrefetchScalarGridSpec(
            num_scalar_prefetch=2, grid=grid,
            in_specs=[pl.BlockSpec((BLOCK_REQ, rows, width), blk),
                      pl.BlockSpec((BLOCK_REQ, shard_len, width), blk),
                      pl.BlockSpec((BLOCK_REQ, shard_len, width), blk)],
            out_specs=pl.BlockSpec((BLOCK_REQ, rows, head_dim + 2), blk)),
    )(start, lengths, spread, keys, values)


def attend_shard(query_sel, keys_sel, values_sel, lengths_sel, offsets_sel, slot_base):
    step_count, request_count, local_kv, group_size, head_dim = query_sel.shape
    query_rows = jnp.transpose(query_sel, (1, 2, 0, 3, 4)).reshape(
        request_count, local_kv, step_count * group_size, head_dim
    )
    blank = jnp.zeros((request_count, step_count * group_size, head_dim), query_sel.dtype)
    spread = jnp.concatenate(
        [
            jnp.concatenate([query_rows[:, k] if j == k else blank for j in range(local_kv)], axis=-1)
            for k in range(local_kv)
        ],
        axis=1,
    )
    start = (slot_base - offsets_sel) % S_CAP
    return cache_attention(start, lengths_sel, spread, keys_sel, values_sel, head_dim)


def local(
    hidden_in,
    lengths,
    request_perm,
    k_cache,
    v_cache,
    attn_gain,
    w_query,
    w_key,
    w_value,
    w_out,
    mlp_gain,
    w_gate,
    w_up,
    w_down,
):
    step_count, request_count, model_width = hidden_in.shape
    row_total = step_count * request_count
    group_size = H // KVH
    local_kv = k_cache.shape[2] // HD
    local_heads = local_kv * group_size
    shard_len = k_cache.shape[1]
    flat_in = hidden_in.reshape(row_total, model_width)
    normed = rms_norm(flat_in, attn_gain)
    positions = lengths[None, :] + jnp.arange(step_count, dtype=jnp.int32)[:, None]
    query_raw = jnp.dot(normed, w_query, preferred_element_type=jnp.float32).reshape(
        step_count, request_count, local_heads, HD
    )
    key_raw = jnp.dot(normed, w_key, preferred_element_type=jnp.float32).reshape(
        step_count, request_count, local_kv, HD
    )
    value_new = (
        jnp.dot(normed, w_value, preferred_element_type=jnp.float32)
        .astype(jnp.bfloat16)
        .reshape(step_count, request_count, local_kv, HD)
    )
    queries = (
        rotate(query_raw, positions)
        .astype(jnp.bfloat16)
        .reshape(step_count, request_count, local_kv, group_size, HD)
    )
    key_new = rotate(key_raw, positions).astype(jnp.bfloat16)
    offsets = request_perm * S_CAP // request_count
    slot_base = lax.axis_index("seq") * shard_len
    packed = attend_shard(queries, k_cache, v_cache, lengths, offsets, slot_base)

    levels = (CORE, ZAX, XAX)
    packed = packed.reshape((2, 4, 4, -1) + packed.shape[1:])
    for level in levels:
        packed = softmax_scatter(level, packed)
    own_shape = (packed.shape[0], local_kv, step_count, group_size)
    top_s = packed[..., HD].reshape(own_shape)
    total_s = packed[..., HD + 1].reshape(own_shape)
    mixed_s = packed[..., :HD].reshape(own_shape + (HD,))
    own_count = top_s.shape[0]
    first_req = ((coord(CORE) * 4 + coord(ZAX)) * 4 + coord(XAX)) * own_count

    def own(x):
        return lax.dynamic_slice_in_dim(x, first_req, own_count, axis=1)

    queries_own = own(queries)
    key_own = own(key_new)
    value_own = own(value_new)
    causal = jnp.arange(step_count)[None, :] <= jnp.arange(step_count)[:, None]
    causal_full = causal[None, None, :, None, :]
    new_scores = (
        jnp.einsum("trkgd,urkd->rktgu", queries_own, key_own, preferred_element_type=jnp.float32)
        * attn_scale
    )
    top_new = jnp.max(jnp.where(causal_full, new_scores, neg_large), axis=-1)
    top_final = jnp.maximum(top_s, top_new)
    new_weights = jnp.where(causal_full, jnp.exp(new_scores - top_final[..., None]), 0.0)
    new_mixed = jnp.einsum(
        "rktgu,urkd->rktgd",
        new_weights.astype(jnp.bfloat16),
        value_own,
        preferred_element_type=jnp.float32,
    )
    weight_cache = jnp.exp(top_s - top_final)
    denominator = total_s * weight_cache + jnp.sum(new_weights, axis=-1)
    heads = (mixed_s * weight_cache[..., None] + new_mixed) / denominator[..., None]
    heads = (
        jnp.transpose(heads, (2, 0, 1, 3, 4))
        .reshape(step_count * own_count, local_heads * HD)
        .astype(jnp.bfloat16)
    )
    attended_part = jnp.dot(heads, w_out, preferred_element_type=jnp.float32).reshape(
        step_count, own_count, model_width
    )
    attended = sum_all_ordered(attended_part.reshape(-1, model_width), YAX)
    hidden_own = lax.dynamic_slice_in_dim(hidden_in, first_req, own_count, axis=1).reshape(
        -1, model_width
    )
    residual = (hidden_own.astype(jnp.float32) + branch_scale * attended).astype(jnp.bfloat16)
    normed_mlp = rms_norm(residual, mlp_gain)

    gather_levels = (XAX, ZAX)
    rows = normed_mlp
    for level in gather_levels:
        rows = gather_rel(rows, level)
    halves = (rows, shifted(rows, CORE, 1))
    block_shape = rows.shape[:-1]
    contract_rows = (((1,), (1,)), ((), ()))

    def feed(half_rows):
        flat = half_rows.reshape(-1, model_width)
        gate = lax.dot_general(flat, w_gate, contract_rows, preferred_element_type=jnp.float32)
        up_proj = lax.dot_general(flat, w_up, contract_rows, preferred_element_type=jnp.float32)
        hidden = (jax.nn.silu(gate) * up_proj).astype(jnp.bfloat16)
        return jnp.dot(hidden, w_down, preferred_element_type=jnp.float32).reshape(
            block_shape + (model_width,)
        )

    feed_forward = feed(halves[0]) + shifted(feed(halves[1]), CORE, 1)
    for level in reversed(gather_levels):
        feed_forward = sum_scatter_rel(feed_forward, level, jnp.bfloat16)
    feed_forward = sum_all_ordered(feed_forward, YAX)
    output = (residual.astype(jnp.float32) + branch_scale * feed_forward).astype(jnp.bfloat16)

    out_rows = output
    for level in gather_levels:
        out_rows = gather_rel(out_rows, level)
    out_halves = (out_rows, shifted(out_rows, CORE, 1))
    own_rows = out_rows.shape[2]
    half_flat = [h.reshape(-1, model_width) for h in out_halves]
    half_count = half_flat[0].shape[0]
    dest = jnp.arange(2 * half_count, dtype=jnp.int32)
    pair = dest % own_count
    dest = dest // own_count
    member = {}
    for level in (XAX, ZAX, CORE):
        member[level] = dest % level[2]
        dest = dest // level[2]
    step_of = dest % step_count
    source = jnp.zeros_like(dest)
    for level in (CORE, ZAX, XAX):
        size = level[2]
        source = source * size + (coord(level) - member[level]) % size
    source = source * own_rows + step_of * own_count + pair
    merged = 0.0
    for kc, flat in enumerate(half_flat):
        cols = kc * half_count + jnp.arange(half_count, dtype=jnp.int32)
        one_hot = (source[:, None] == cols[None, :]).astype(flat.dtype)
        merged = merged + jnp.dot(one_hot, flat, preferred_element_type=jnp.float32)
    hidden_out = merged.astype(jnp.bfloat16).reshape(step_count, request_count, model_width)
    key_out = key_new.reshape(step_count, request_count, local_kv * HD)
    value_out = value_new.reshape(step_count, request_count, local_kv * HD)
    return (hidden_out, key_out, value_out)


def solution(mesh):
    placed = (
        P(),
        P(),
        P(),
        P(None, "seq", "tp"),
        P(None, "seq", "tp"),
        P(),
        P(None, "tp"),
        P(None, "tp"),
        P(None, "tp"),
        P("tp", None),
        P(),
        P(("seq", "tp"), None),
        P(("seq", "tp"), None),
        P(("seq", "tp"), None),
    )
    return jax.shard_map(
        local,
        mesh=mesh,
        in_specs=placed,
        out_specs=(P(), P(None, None, "tp"), P(None, None, "tp")),
        check_vma=False,
    )
```

```python
import math

import jax
import jax.numpy as jnp
from jax import lax
from jax.experimental import pallas as pl
from jax.experimental.pallas import tpu as pltpu
from jax.sharding import PartitionSpec as P

H = 32
KVH = 8
HD = 64
S_CAP = 16384


norm_eps = 1e-05
rope_theta = 10000000.0
attn_scale = 0.015625
branch_scale = 0.5
neg_large = -1e30

CORE = ("seq", 1, 2)
ZAX = ("seq", 2, 4)
XAX = ("seq", 8, 4)
YAX = ("tp", 1, 4)
AXIS_SIZE = {"seq": 32, "tp": 4}


def coord(level):
    axis, stride, size = level
    return (lax.axis_index(axis) // stride) % size


def shift_perm(level, d):
    axis, stride, size = level
    pairs = []
    for i in range(AXIS_SIZE[axis]):
        c = (i // stride) % size
        pairs.append((i, i + ((c + d) % size - c) * stride))
    return pairs


def shifted(x, level, d):
    return lax.ppermute(x, level[0], shift_perm(level, d))


def take(x, index):
    return lax.dynamic_index_in_dim(x, index, axis=0, keepdims=False)


def softmax_scatter(level, packed):
    size = level[2]
    c = coord(level)
    parts = [take(packed, c)]
    for d in range(1, size):
        parts.append(shifted(take(packed, (c + d) % size), level, d))
    head_dim = packed.shape[-1] - 2
    top_all = parts[0][..., head_dim]
    for p in parts[1:]:
        top_all = jnp.maximum(top_all, p[..., head_dim])
    total_all = 0.0
    mixed_all = 0.0
    for p in parts:
        factor = jnp.exp(p[..., head_dim] - top_all)
        total_all = total_all + p[..., head_dim + 1] * factor
        mixed_all = mixed_all + p[..., :head_dim] * factor[..., None]
    return jnp.concatenate([mixed_all, top_all[..., None], total_all[..., None]], axis=-1)


def sum_scatter_abs(x, level):
    size = level[2]
    c = coord(level)
    acc = take(x, c)
    for d in range(1, size):
        acc = acc + shifted(take(x, (c + d) % size), level, d)
    return acc


def sum_all_ordered(x, level):
    size = level[2]
    c = coord(level)
    parts = [x] + [shifted(x, level, d) for d in range(1, size)]
    total = None
    for m in range(size):
        part = parts[0]
        for d in range(1, size):
            part = jnp.where((c - d) % size == m, parts[d], part)
        total = part if total is None else total + part
    return total


def gather_rel(x, level):
    size = level[2]
    parts = [x] + [shifted(x, level, d) for d in range(1, size)]
    return jnp.stack(parts, axis=0)


def sum_scatter_rel(x, level, wire):
    size = level[2]
    acc = x[0]
    for d in range(1, size):
        acc = acc + shifted(x[size - d].astype(wire), level, d).astype(acc.dtype)
    return acc


def rms_norm(values, gain_vector):
    floats = values.astype(jnp.float32)
    square_mean = jnp.mean(floats * floats, axis=-1, keepdims=True)
    return (floats * lax.rsqrt(square_mean + norm_eps) * gain_vector.astype(jnp.float32)).astype(
        jnp.bfloat16
    )


def rotate(vectors, positions):
    half_size = vectors.shape[-1] // 2
    inverse = jnp.exp(
        jnp.arange(half_size, dtype=jnp.float32) * (-2.0 * math.log(rope_theta) / vectors.shape[-1])
    )
    angles = positions.astype(jnp.float32)[..., None] * inverse
    cosine = jnp.cos(angles)[..., None, :]
    sine = jnp.sin(angles)[..., None, :]
    first_half = vectors[..., :half_size]
    second_half = vectors[..., half_size:]
    return jnp.concatenate(
        [first_half * cosine - second_half * sine, second_half * cosine + first_half * sine],
        axis=-1,
    )


BLOCK_REQ = 4


def cache_kernel(start_ref, len_ref, q_ref, k_ref, v_ref, packed_ref):
    block = pl.program_id(0)
    rows = q_ref.shape[1]
    half = rows // 2
    head_dim = packed_ref.shape[2] - 2
    shard_len = k_ref.shape[1]
    slots = lax.broadcasted_iota(jnp.int32, (1, shard_len), 1)
    for i in range(q_ref.shape[0]):
        r = block * q_ref.shape[0] + i
        rel = slots + start_ref[r]
        rel = jnp.where(rel >= S_CAP, rel - S_CAP, rel)
        live = rel < len_ref[r]
        scores = lax.dot_general(q_ref[i], k_ref[i], (((1,), (1,)), ((), ())),
                                 preferred_element_type=jnp.float32) * attn_scale
        top = jnp.max(jnp.where(live, scores, neg_large), axis=-1, keepdims=True)
        weights = jnp.where(live, jnp.exp(scores - top), 0.0)
        packed_ref[i, :, head_dim:head_dim + 1] = top
        packed_ref[i, :, head_dim + 1:head_dim + 2] = jnp.sum(weights, axis=-1, keepdims=True)
        mixed = jnp.dot(weights.astype(jnp.bfloat16), v_ref[i], preferred_element_type=jnp.float32)
        packed_ref[i, 0:half, 0:head_dim] = mixed[0:half, 0:head_dim]
        packed_ref[i, half:rows, 0:head_dim] = mixed[half:rows, head_dim:2 * head_dim]


def cache_attention(start, lengths, spread, keys, values, head_dim):
    req, rows, width = spread.shape
    shard_len = keys.shape[1]
    grid = (req // BLOCK_REQ,)
    def blk(b, s, l):
        return (b, 0, 0)
    return pl.pallas_call(
        cache_kernel,
        out_shape=jax.ShapeDtypeStruct((req, rows, head_dim + 2), jnp.float32),
        grid_spec=pltpu.PrefetchScalarGridSpec(
            num_scalar_prefetch=2, grid=grid,
            in_specs=[pl.BlockSpec((BLOCK_REQ, rows, width), blk),
                      pl.BlockSpec((BLOCK_REQ, shard_len, width), blk),
                      pl.BlockSpec((BLOCK_REQ, shard_len, width), blk)],
            out_specs=pl.BlockSpec((BLOCK_REQ, rows, head_dim + 2), blk)),
    )(start, lengths, spread, keys, values)


def attend_shard(query_sel, keys_sel, values_sel, lengths_sel, offsets_sel, slot_base):
    step_count, request_count, local_kv, group_size, head_dim = query_sel.shape
    query_rows = jnp.transpose(query_sel, (1, 2, 0, 3, 4)).reshape(
        request_count, local_kv, step_count * group_size, head_dim
    )
    blank = jnp.zeros((request_count, step_count * group_size, head_dim), query_sel.dtype)
    spread = jnp.concatenate(
        [
            jnp.concatenate([query_rows[:, k] if j == k else blank for j in range(local_kv)], axis=-1)
            for k in range(local_kv)
        ],
        axis=1,
    )
    start = (slot_base - offsets_sel) % S_CAP
    return cache_attention(start, lengths_sel, spread, keys_sel, values_sel, head_dim)


def local(
    hidden_in,
    lengths,
    request_perm,
    k_cache,
    v_cache,
    attn_gain,
    w_query,
    w_key,
    w_value,
    w_out,
    mlp_gain,
    w_gate,
    w_up,
    w_down,
):
    step_count, request_count, model_width = hidden_in.shape
    row_total = step_count * request_count
    group_size = H // KVH
    local_kv = k_cache.shape[2] // HD
    local_heads = local_kv * group_size
    shard_len = k_cache.shape[1]
    flat_in = hidden_in.reshape(row_total, model_width)
    normed = rms_norm(flat_in, attn_gain)
    positions = lengths[None, :] + jnp.arange(step_count, dtype=jnp.int32)[:, None]
    query_raw = jnp.dot(normed, w_query, preferred_element_type=jnp.float32).reshape(
        step_count, request_count, local_heads, HD
    )
    key_raw = jnp.dot(normed, w_key, preferred_element_type=jnp.float32).reshape(
        step_count, request_count, local_kv, HD
    )
    value_new = (
        jnp.dot(normed, w_value, preferred_element_type=jnp.float32)
        .astype(jnp.bfloat16)
        .reshape(step_count, request_count, local_kv, HD)
    )
    queries = (
        rotate(query_raw, positions)
        .astype(jnp.bfloat16)
        .reshape(step_count, request_count, local_kv, group_size, HD)
    )
    key_new = rotate(key_raw, positions).astype(jnp.bfloat16)
    offsets = request_perm * S_CAP // request_count
    slot_base = lax.axis_index("seq") * shard_len
    packed = attend_shard(queries, k_cache, v_cache, lengths, offsets, slot_base)

    levels = (CORE, ZAX, XAX)
    packed = packed.reshape((2, 4, 4, -1) + packed.shape[1:])
    for level in levels:
        packed = softmax_scatter(level, packed)
    own_shape = (packed.shape[0], local_kv, step_count, group_size)
    top_s = packed[..., HD].reshape(own_shape)
    total_s = packed[..., HD + 1].reshape(own_shape)
    mixed_s = packed[..., :HD].reshape(own_shape + (HD,))
    own_count = top_s.shape[0]
    first_req = ((coord(CORE) * 4 + coord(ZAX)) * 4 + coord(XAX)) * own_count

    def own(x):
        return lax.dynamic_slice_in_dim(x, first_req, own_count, axis=1)

    queries_own = own(queries)
    key_own = own(key_new)
    value_own = own(value_new)
    causal = jnp.arange(step_count)[None, :] <= jnp.arange(step_count)[:, None]
    causal_full = causal[None, None, :, None, :]
    new_scores = (
        jnp.einsum("trkgd,urkd->rktgu", queries_own, key_own, preferred_element_type=jnp.float32)
        * attn_scale
    )
    top_new = jnp.max(jnp.where(causal_full, new_scores, neg_large), axis=-1)
    top_final = jnp.maximum(top_s, top_new)
    new_weights = jnp.where(causal_full, jnp.exp(new_scores - top_final[..., None]), 0.0)
    new_mixed = jnp.einsum(
        "rktgu,urkd->rktgd",
        new_weights.astype(jnp.bfloat16),
        value_own,
        preferred_element_type=jnp.float32,
    )
    weight_cache = jnp.exp(top_s - top_final)
    denominator = total_s * weight_cache + jnp.sum(new_weights, axis=-1)
    heads = (mixed_s * weight_cache[..., None] + new_mixed) / denominator[..., None]
    heads = (
        jnp.transpose(heads, (2, 0, 1, 3, 4))
        .reshape(step_count * own_count, local_heads * HD)
        .astype(jnp.bfloat16)
    )
    attended_part = jnp.dot(heads, w_out, preferred_element_type=jnp.float32).reshape(
        step_count, own_count, model_width
    )
    attended = sum_all_ordered(attended_part.reshape(-1, model_width), YAX)
    hidden_own = lax.dynamic_slice_in_dim(hidden_in, first_req, own_count, axis=1).reshape(
        -1, model_width
    )
    residual = (hidden_own.astype(jnp.float32) + branch_scale * attended).astype(jnp.bfloat16)
    normed_mlp = rms_norm(residual, mlp_gain)

    gather_levels = (XAX, ZAX)
    rows = normed_mlp
    for level in gather_levels:
        rows = gather_rel(rows, level)
    halves = (rows, shifted(rows, CORE, 1))
    block_shape = rows.shape[:-1]
    contract_rows = (((1,), (1,)), ((), ()))

    def feed(half_rows):
        flat = half_rows.reshape(-1, model_width)
        gate = lax.dot_general(flat, w_gate, contract_rows, preferred_element_type=jnp.float32)
        up_proj = lax.dot_general(flat, w_up, contract_rows, preferred_element_type=jnp.float32)
        hidden = (jax.nn.silu(gate) * up_proj).astype(jnp.bfloat16)
        return jnp.dot(hidden, w_down, preferred_element_type=jnp.float32).reshape(
            block_shape + (model_width,)
        )

    feed_forward = feed(halves[0]) + shifted(feed(halves[1]), CORE, 1)
    for level in reversed(gather_levels):
        feed_forward = sum_scatter_rel(feed_forward, level, jnp.bfloat16)
    feed_forward = sum_all_ordered(feed_forward, YAX)
    output = (residual.astype(jnp.float32) + branch_scale * feed_forward).astype(jnp.bfloat16)

    out_rows = output
    for level in gather_levels:
        out_rows = gather_rel(out_rows, level)
    out_halves = (out_rows, shifted(out_rows, CORE, 1))
    own_rows = out_rows.shape[2]
    half_flat = [h.reshape(-1, model_width) for h in out_halves]
    half_count = half_flat[0].shape[0]
    dest = jnp.arange(2 * half_count, dtype=jnp.int32)
    pair = dest % own_count
    dest = dest // own_count
    member = {}
    for level in (XAX, ZAX, CORE):
        member[level] = dest % level[2]
        dest = dest // level[2]
    step_of = dest % step_count
    source = jnp.zeros_like(dest)
    for level in (CORE, ZAX, XAX):
        size = level[2]
        source = source * size + (coord(level) - member[level]) % size
    source = source * own_rows + step_of * own_count + pair
    merged = 0.0
    for kc, flat in enumerate(half_flat):
        cols = kc * half_count + jnp.arange(half_count, dtype=jnp.int32)
        one_hot = (source[:, None] == cols[None, :]).astype(flat.dtype)
        merged = merged + jnp.dot(one_hot, flat, preferred_element_type=jnp.float32)
    hidden_out = merged.astype(jnp.bfloat16).reshape(step_count, request_count, model_width)
    key_out = key_new.reshape(step_count, request_count, local_kv * HD)
    value_out = value_new.reshape(step_count, request_count, local_kv * HD)
    return (hidden_out, key_out, value_out)


def solution(mesh):
    placed = (
        P(),
        P(),
        P(),
        P(None, "seq", "tp"),
        P(None, "seq", "tp"),
        P(),
        P(None, "tp"),
        P(None, "tp"),
        P(None, "tp"),
        P("tp", None),
        P(),
        P(("seq", "tp"), None),
        P(("seq", "tp"), None),
        P(("seq", "tp"), None),
    )
    return jax.shard_map(
        local,
        mesh=mesh,
        in_specs=placed,
        out_specs=(P(), P(None, None, "tp"), P(None, None, "tp")),
        check_vma=False,
    )
```
